128 devices in a mesh: req: 16 (over x, y), vocab: 8 (over z, core).
Axes of the slice: x: 4, y: 4, z: 4, core: 2. Of those that a mesh axis runs over, the one named last changes fastest.
Arguments:
- hidden: bfloat16 [64, 128, 2048], P('req'), may hold values from -1000 to 1000
- gain: float32 [2048], replicated, may hold values from 0.5 to 1.5
- embedding: bfloat16 [76800, 2048], P('vocab', 'req'), may hold values from -16 to 16
- targets: int32 [64, 128], P('req'), may hold values from 0 to 76799
- span_start: int32 [64], P('req'), may hold values from 0 to 127, as said below
- span_len: int32 [64], P('req'), may hold values from 1 to 128
- deal_order: int32 [64], replicated, may hold values from 0 to 63, as said below
Outputs:
- logprob: float32 [64, 128], P('req')
- entropy: float32 [64, 128], P('req')
The draws below stay inside these ranges and needn't reach their ends.
Inputs may be any that keep to these rules, and one draw needn't show every extreme that they name: deal_order is a permutation of the requests; the span lengths of the 4 requests dealt to one group add up to at most 224, exactly 224 for some group. span_start + span_len <= 128 for every request.
All inputs are finite; a program needn't handle non-finite values.
Results may differ from the reference program's by a relative error of at most 0.0029.
Values may be sent and summed in bfloat16 or wider, within the bound.
No kernel may reach another device: no remote copies, remote signals or barrier semaphores. Data moves between devices by JAX's collectives and lax.ppermute only.
A program may use at most 128 MiB of HBM per device.

```python
import math
import jax
import jax.numpy as jnp
from jax import lax

D = 2048
REQ_DEV = 4
SLOT = 128
CAP = 224
REQS = 64
VOCAB = 76800
N_REQ = 16


def span_plan(key):
    base_key = jax.random.fold_in(key, 101)
    key_list = jax.random.split(base_key, 8)
    group_count = REQS // REQ_DEV
    short_most = SLOT // 4
    slot_ids = jnp.arange(REQS, dtype=jnp.int32)
    group_of = slot_ids // REQ_DEV
    entry_pos = slot_ids % REQ_DEV
    leader_pos = jax.random.randint(key_list[0], (group_count,), 0, REQ_DEV)
    is_long = entry_pos == leader_pos[group_of]
    long_len = jax.random.randint(key_list[1], (REQS,), 3 * SLOT // 4, SLOT + 1)
    short_len = jax.random.randint(key_list[2], (REQS,), 1, short_most + 1)
    full_group = jax.random.randint(key_list[3], (), 0, group_count)
    tiny_group = (full_group + 1) % group_count
    tiny_entry = (leader_pos[tiny_group] + 1) % REQ_DEV
    short_len = jnp.where(group_of == full_group, short_most, short_len)
    short_len = jnp.where((group_of == tiny_group) & (entry_pos == tiny_entry), 1, short_len)
    long_len = jnp.where(group_of == full_group, SLOT, long_len)
    dealt_len = jnp.where(is_long, long_len, short_len)
    rank_order = jax.random.permutation(key_list[4], REQS).astype(jnp.int32)
    ordered = jnp.argsort(jnp.where(is_long, rank_order, rank_order + REQS)).astype(jnp.int32)
    mix_order = jax.random.permutation(key_list[5], REQS - REQ_DEV)
    tail_part = ordered[REQ_DEV:][mix_order]
    sequence = jnp.concatenate([ordered[:REQ_DEV], tail_part])
    first_group = jax.random.randint(key_list[6], (), 0, group_count)
    owner_slot = (slot_ids + first_group * REQ_DEV) % REQS
    dealt_pos = jnp.zeros((REQS,), jnp.int32).at[owner_slot].set(sequence)
    span_length = dealt_len[dealt_pos]
    span_offset = jax.random.randint(key_list[7], (REQS,), 0, SLOT + 1) % (SLOT - span_length + 1)
    span_offset = jnp.where(span_length == 1, SLOT - 1, span_offset)
    return (dealt_pos.astype(jnp.int32), span_offset.astype(jnp.int32), span_length.astype(jnp.int32))


def draw_deal_order(key, part):
    return span_plan(key)[0]


def draw_span_start(key, part):
    return span_plan(key)[1]


def draw_span_len(key, part):
    return span_plan(key)[2]


def embed_row(key, word_index):
    row_key = jax.random.fold_in(jax.random.fold_in(key, 303), word_index)
    return jnp.clip(jax.random.normal(row_key, (D,)), -6.0, 6.0) * (3.0 / math.sqrt(D))


def draw_embedding(key, part):
    table = jax.vmap(lambda word_index: embed_row(key, word_index))(jnp.arange(VOCAB, dtype=jnp.int32))
    return jnp.clip(table, -16.0, 16.0).astype(jnp.bfloat16)


def draw_hidden(key, part):
    base_key = jax.random.fold_in(key, 202)
    key_list = jax.random.split(base_key, 4)
    column_scale = jnp.exp(jax.random.uniform(key_list[0], (D,), minval=0.0, maxval=math.log(10.0)))
    token_scale = jnp.exp(jax.random.uniform(key_list[1], (REQS, SLOT, 1), minval=0.0, maxval=math.log(10.0)))
    values = jnp.clip(jax.random.normal(key_list[3], (REQS, SLOT, D)), -4.0, 4.0) * column_scale * token_scale
    return jnp.clip(values, -1000.0, 1000.0).astype(jnp.bfloat16)


def with_ends(array, key, low, largest):
    spot = [jax.random.randint(jax.random.fold_in(key, axis), (), 0, length) for axis, length in enumerate(array.shape)]
    longest = array.shape.index(max(array.shape))
    beside = spot[:longest] + [(spot[longest] + 1) % array.shape[longest]] + spot[longest + 1:]
    return array.at[tuple(spot)].set(low).at[tuple(beside)].set(largest)


def setup_inputs(seed: int = 0) -> dict:
    seeds = jax.random.split(jax.random.key(seed), 8)
    return {
        "hidden": draw_hidden(jax.random.fold_in(seeds[7], 71), 0),
        "gain": jnp.clip(1.0 + 0.1 * jax.random.normal(seeds[1], (D,), jnp.float32), 0.5, 1.5),
        "embedding": draw_embedding(jax.random.fold_in(seeds[7], 71), 0),
        "targets": with_ends(jax.random.randint(seeds[3], (REQS, SLOT), 0, VOCAB), jax.random.fold_in(seeds[3], 1), 0, VOCAB - 1).astype(jnp.int32),
        "span_start": draw_span_start(jax.random.fold_in(seeds[7], 71), 0),
        "span_len": draw_span_len(jax.random.fold_in(seeds[7], 71), 0),
        "deal_order": draw_deal_order(jax.random.fold_in(seeds[7], 71), 0),
    }


eps = 1e-06

def compact_plan(row_base, lengths, capacity):
    offsets = jnp.cumsum(lengths) - lengths
    counter = jnp.arange(capacity, dtype=jnp.int32)
    member = lax.optimization_barrier(jnp.sum((counter[:, None] >= offsets[None, :]).astype(jnp.int32), axis=1)) - 1
    member_hot = (member[:, None] == jnp.arange(lengths.shape[0], dtype=jnp.int32)[None, :]).astype(jnp.int32)
    row_index = lax.optimization_barrier(jnp.sum(member_hot * (row_base - offsets)[None, :], axis=1)) + counter
    in_span = counter < jnp.sum(lengths)
    return (row_index.astype(jnp.int32), in_span)

def normalize(rows, gain):
    wide_rows = rows.astype(jnp.float32)
    scale = lax.rsqrt(lax.optimization_barrier(jnp.mean(wide_rows * wide_rows, axis=1, keepdims=True)) + eps)
    return (wide_rows * scale * gain).astype(jnp.bfloat16)

def reference(hidden, gain, embedding, targets, span_start, span_len, deal_order):
    total = deal_order.shape[0]
    positions = jnp.arange(total, dtype=jnp.int32)
    source_of = lax.optimization_barrier(jnp.sum(jnp.where(deal_order[None, :] == positions[:, None], positions[None, :], 0), axis=1)).astype(jnp.int32)
    flat_hidden = hidden.reshape(total * SLOT, D)
    flat_targets = targets.reshape(total * SLOT)
    vocab_ids = jnp.arange(VOCAB, dtype=jnp.int32)

    def one_group(group):
        members = lax.dynamic_slice_in_dim(source_of, (group * REQ_DEV).astype(jnp.int32), REQ_DEV)
        lengths = span_len[members]
        row_base = members * SLOT + span_start[members]
        row_index, in_span = compact_plan(row_base, lengths, CAP)
        safe_index = jnp.where(in_span, row_index, 0)
        normed = normalize(flat_hidden[safe_index], gain)
        target_ids = jnp.where(in_span, flat_targets[safe_index], -1)
        logits = lax.dot_general(normed, embedding, (((1,), (1,)), ((), ())), preferred_element_type=jnp.float32)
        row_top = lax.optimization_barrier(jnp.max(logits, axis=1))
        shifted = logits - row_top[:, None]
        weights = jnp.exp(shifted)
        row_mass = lax.optimization_barrier(jnp.sum(weights, axis=1))
        row_spread = lax.optimization_barrier(jnp.sum(weights * shifted, axis=1))
        row_target = lax.optimization_barrier(jnp.sum(jnp.where(vocab_ids[None, :] == target_ids[:, None], logits, 0.0), axis=1))
        log_mass = jnp.log(row_mass)
        group_logprob = jnp.where(in_span, row_target - row_top - log_mass, 0.0)
        group_entropy = jnp.where(in_span, log_mass - row_spread / row_mass, 0.0)
        spot = jnp.where(in_span, row_index, total * SLOT)
        return (spot, group_logprob, group_entropy)
    spots, logprobs, entropies = lax.map(one_group, jnp.arange(N_REQ, dtype=jnp.int32))
    flat_spots = spots.reshape(-1)
    logprob = jnp.zeros((total * SLOT,), jnp.float32).at[flat_spots].set(logprobs.reshape(-1), mode='drop')
    entropy = jnp.zeros((total * SLOT,), jnp.float32).at[flat_spots].set(entropies.reshape(-1), mode='drop')
    return (logprob.reshape(total, SLOT), entropy.reshape(total, SLOT))
```

```python
import functools

import jax
import jax.numpy as jnp
from jax import lax
from jax.sharding import PartitionSpec as P

CAP = 224


eps = 1e-06


def compact_plan(row_base, lengths, capacity):
    offsets = jnp.cumsum(lengths) - lengths
    counter = jnp.arange(capacity, dtype=jnp.int32)
    member = jnp.sum((counter[:, None] >= offsets[None, :]).astype(jnp.int32), axis=1) - 1
    member_hot = (member[:, None] == jnp.arange(lengths.shape[0], dtype=jnp.int32)[None, :]).astype(
        jnp.int32
    )
    row_index = jnp.sum(member_hot * (row_base - offsets)[None, :], axis=1) + counter
    in_span = counter < jnp.sum(lengths)
    return (row_index, in_span)


def normalize(rows, gain):
    wide_rows = rows.astype(jnp.float32)
    scale = lax.rsqrt(jnp.mean(wide_rows * wide_rows, axis=-1, keepdims=True) + eps)
    return (wide_rows * scale * gain).astype(jnp.bfloat16)


def shards(n_voc, hidden, gain, embedding, targets, span_start, span_len, deal_order):
    per_dev = hidden.shape[0]
    slot_len = hidden.shape[1]
    width = hidden.shape[2]
    total = deal_order.shape[0]
    n_req = total // per_dev
    voc_local = embedding.shape[0]
    piece = voc_local // n_req
    half = width // 2
    here = lax.axis_index("req")
    vhere = lax.axis_index("vocab")
    core = vhere % 2
    positions = jnp.arange(total, dtype=jnp.int32)
    source_of = jnp.sum(
        jnp.where(deal_order[None, :] == positions[:, None], positions[None, :], 0), axis=1
    )

    emb_piece = lax.all_to_all(embedding, "req", split_axis=0, concat_axis=1, tiled=True)

    meta = jnp.concatenate([targets, span_start[:, None], span_len[:, None]], axis=1)
    meta_all = lax.all_gather(meta, "req", axis=0, tiled=True)
    all_targets = meta_all[:, :slot_len]
    all_starts = meta_all[:, slot_len]
    all_lengths = meta_all[:, slot_len + 1]

    normed_home = normalize(hidden, gain)
    my_half = lax.dynamic_slice_in_dim(normed_home, core * half, half, axis=2)
    spread_rows = lax.all_to_all(my_half, "req", split_axis=1, concat_axis=0, tiled=True)
    dealt_rows = jnp.take(spread_rows, source_of, axis=0)
    home_rows = lax.all_to_all(dealt_rows, "req", split_axis=0, concat_axis=1, tiled=True)

    my_slots = here * per_dev + jnp.arange(per_dev, dtype=jnp.int32)
    members = jnp.take(source_of, my_slots)
    lengths = jnp.take(all_lengths, members)
    starts = jnp.take(all_starts, members)
    row_base = jnp.arange(per_dev, dtype=jnp.int32) * slot_len + starts
    row_index, in_span = compact_plan(row_base, lengths, CAP)
    safe_index = jnp.where(in_span, row_index, 0)
    compact_half = jnp.take(home_rows.reshape(per_dev * slot_len, half), safe_index, axis=0)

    rows_mine = lax.all_gather(compact_half, "req", axis=0, tiled=True)
    pairs = [(2 * k + j, 2 * k + 1 - j) for k in range(n_voc // 2) for j in range(2)]
    rows_other = lax.ppermute(rows_mine, "vocab", pairs)

    emb_mine = lax.dynamic_slice_in_dim(emb_piece, core * half, half, axis=1)
    emb_other = lax.dynamic_slice_in_dim(emb_piece, (1 - core) * half, half, axis=1)
    dims = (((1,), (1,)), ((), ()))
    logits = lax.dot_general(rows_mine, emb_mine, dims, preferred_element_type=jnp.float32)
    logits = logits + lax.dot_general(rows_other, emb_other, dims, preferred_element_type=jnp.float32)

    dealt_members = source_of.reshape(n_req, per_dev)
    dealt_lengths = jnp.take(all_lengths, dealt_members)
    dealt_base = dealt_members * slot_len + jnp.take(all_starts, dealt_members)
    all_index, all_in = jax.vmap(lambda b, l: compact_plan(b, l, CAP))(dealt_base, dealt_lengths)
    all_index = jnp.where(all_in, all_index, 0).reshape(-1)
    target_ids = jnp.take(all_targets.reshape(-1), all_index)

    local_top = jnp.max(logits, axis=1)
    shifted = logits - local_top[:, None]
    weights = jnp.exp(shifted)
    local_mass = jnp.sum(weights, axis=1)
    local_spread = jnp.sum(weights * shifted, axis=1)
    local_ids = target_ids - (vhere * voc_local + here * piece)
    local_target = jnp.sum(
        jnp.where(jnp.arange(piece, dtype=jnp.int32)[None, :] == local_ids[:, None], logits, 0.0),
        axis=1,
    )
    both = ("req", "vocab")
    row_top = lax.pmax(local_top, both)
    factor = jnp.exp(local_top - row_top)
    row_mass, row_spread, row_target = lax.psum(
        (
            factor * local_mass,
            factor * (local_spread + (local_top - row_top) * local_mass),
            local_target,
        ),
        both,
    )
    log_mass = jnp.log(row_mass)
    all_logprob = row_target - row_top - log_mass
    all_entropy = log_mass - row_spread / row_mass

    offsets = (jnp.cumsum(dealt_lengths, axis=1) - dealt_lengths).reshape(-1)
    my_reqs = here * per_dev + jnp.arange(per_dev, dtype=jnp.int32)
    my_deal = jnp.take(deal_order, my_reqs)
    my_start = jnp.take(all_starts, my_reqs)
    my_len = jnp.take(all_lengths, my_reqs)
    pos = jnp.arange(slot_len, dtype=jnp.int32)[None, :]
    inside = (pos >= my_start[:, None]) & (pos < (my_start + my_len)[:, None])
    flat = (my_deal // per_dev)[:, None] * CAP + jnp.take(offsets, my_deal)[:, None] + pos - my_start[:, None]
    flat = jnp.where(inside, flat, 0)
    out_logprob = jnp.where(inside, jnp.take(all_logprob, flat), 0.0)
    out_entropy = jnp.where(inside, jnp.take(all_entropy, flat), 0.0)
    return (out_logprob, out_entropy)


def solution(mesh):
    in_specs = (
        P("req", None, None),
        P(),
        P("vocab", "req"),
        P("req", None),
        P("req"),
        P("req"),
        P(),
    )
    out_specs = (P("req", None), P("req", None))
    body = functools.partial(shards, mesh.shape["vocab"])
    return jax.shard_map(body, mesh=mesh, in_specs=in_specs, out_specs=out_specs, check_vma=False)
```

```python
import functools

import jax
import jax.numpy as jnp
from jax import lax
from jax.sharding import PartitionSpec as P

CAP = 224


eps = 1e-06


def compact_plan(row_base, lengths, capacity):
    offsets = jnp.cumsum(lengths) - lengths
    counter = jnp.arange(capacity, dtype=jnp.int32)
    member = jnp.sum((counter[:, None] >= offsets[None, :]).astype(jnp.int32), axis=1) - 1
    member_hot = (member[:, None] == jnp.arange(lengths.shape[0], dtype=jnp.int32)[None, :]).astype(
        jnp.int32
    )
    row_index = jnp.sum(member_hot * (row_base - offsets)[None, :], axis=1) + counter
    in_span = counter < jnp.sum(lengths)
    return (row_index, in_span)


def normalize(rows, gain):
    wide_rows = rows.astype(jnp.float32)
    scale = lax.rsqrt(jnp.mean(wide_rows * wide_rows, axis=-1, keepdims=True) + eps)
    return (wide_rows * scale * gain).astype(jnp.bfloat16)


def shards(n_voc, hidden, gain, embedding, targets, span_start, span_len, deal_order):
    per_dev = hidden.shape[0]
    slot_len = hidden.shape[1]
    width = hidden.shape[2]
    total = deal_order.shape[0]
    n_req = total // per_dev
    voc_local = embedding.shape[0]
    piece = voc_local // n_req
    half = width // 2
    here = lax.axis_index("req")
    vhere = lax.axis_index("vocab")
    core = vhere % 2
    positions = jnp.arange(total, dtype=jnp.int32)
    source_of = jnp.sum(
        jnp.where(deal_order[None, :] == positions[:, None], positions[None, :], 0), axis=1
    )

    emb_piece = lax.all_to_all(embedding, "req", split_axis=0, concat_axis=1, tiled=True)

    meta = jnp.concatenate([targets, span_start[:, None], span_len[:, None]], axis=1)
    meta_all = lax.all_gather(meta.astype(jnp.float32), "req", axis=0, tiled=True).astype(jnp.int32)
    all_targets = meta_all[:, :slot_len]
    all_starts = meta_all[:, slot_len]
    all_lengths = meta_all[:, slot_len + 1]

    normed_home = normalize(hidden, gain)
    my_half = lax.dynamic_slice_in_dim(normed_home, core * half, half, axis=2)
    spread_rows = lax.all_to_all(my_half, "req", split_axis=1, concat_axis=0, tiled=True)
    dealt_rows = jnp.take(spread_rows, source_of, axis=0)
    home_rows = lax.all_to_all(dealt_rows, "req", split_axis=0, concat_axis=1, tiled=True)

    my_slots = here * per_dev + jnp.arange(per_dev, dtype=jnp.int32)
    members = jnp.take(source_of, my_slots)
    lengths = jnp.take(all_lengths, members)
    starts = jnp.take(all_starts, members)
    row_base = jnp.arange(per_dev, dtype=jnp.int32) * slot_len + starts
    row_index, in_span = compact_plan(row_base, lengths, CAP)
    safe_index = jnp.where(in_span, row_index, 0)
    compact_half = jnp.take(home_rows.reshape(per_dev * slot_len, half), safe_index, axis=0)

    rows_mine = lax.all_gather(compact_half, "req", axis=0, tiled=True)
    pairs = [(2 * k + j, 2 * k + 1 - j) for k in range(n_voc // 2) for j in range(2)]
    rows_other = lax.ppermute(rows_mine, "vocab", pairs)

    emb_mine = lax.dynamic_slice_in_dim(emb_piece, core * half, half, axis=1)
    emb_other = lax.dynamic_slice_in_dim(emb_piece, (1 - core) * half, half, axis=1)
    dims = (((1,), (1,)), ((), ()))
    logits = lax.dot_general(rows_mine, emb_mine, dims, preferred_element_type=jnp.float32)
    logits = logits + lax.dot_general(rows_other, emb_other, dims, preferred_element_type=jnp.float32)

    dealt_members = source_of.reshape(n_req, per_dev)
    dealt_lengths = jnp.take(all_lengths, dealt_members)
    dealt_offsets = jnp.cumsum(dealt_lengths, axis=1) - dealt_lengths
    dealt_starts = jnp.take(all_starts, dealt_members)
    padded_targets = jnp.pad(jnp.take(all_targets, source_of, axis=0), ((0, 0), (CAP, CAP)))
    window_at = (dealt_starts - dealt_offsets + CAP).reshape(-1)
    windows = jax.vmap(lambda row, at: lax.dynamic_slice_in_dim(row, at, CAP))(padded_targets, window_at)
    counter = jnp.arange(CAP, dtype=jnp.int32)
    in_member = (counter[None, None, :] >= dealt_offsets[:, :, None]) & (
        counter[None, None, :] < (dealt_offsets + dealt_lengths)[:, :, None]
    )
    target_ids = jnp.sum(jnp.where(in_member, windows.reshape(n_req, per_dev, CAP), 0), axis=1).reshape(-1)

    local_top = jnp.max(logits, axis=1)
    shifted = logits - local_top[:, None]
    weights = jnp.exp(shifted)
    local_mass = jnp.sum(weights, axis=1)
    local_spread = jnp.sum(weights * shifted, axis=1)
    local_ids = target_ids - (vhere * voc_local + here * piece)
    local_target = jnp.sum(
        jnp.where(jnp.arange(piece, dtype=jnp.int32)[None, :] == local_ids[:, None], logits, 0.0),
        axis=1,
    )

    def merge(stats):
        top_each, mass_each, spread_each, target_each = stats[:, 0], stats[:, 1], stats[:, 2], stats[:, 3]
        top = jnp.max(top_each, axis=0)
        gap = top_each - top[None, :]
        factor = jnp.exp(gap)
        mass = jnp.sum(factor * mass_each, axis=0)
        spread = jnp.sum(factor * (spread_each + gap * mass_each), axis=0)
        return jnp.stack([top, mass, spread, jnp.sum(target_each, axis=0)])

    local_stats = jnp.stack([local_top, local_mass, local_spread, local_target]).reshape(4, n_req, CAP)
    by_req = lax.all_to_all(local_stats.transpose(1, 0, 2), "req", split_axis=0, concat_axis=0, tiled=True)
    group_stats = merge(lax.all_gather(merge(by_req), "vocab", axis=0))
    row_top, row_mass, row_spread, row_target = group_stats[0], group_stats[1], group_stats[2], group_stats[3]
    log_mass = jnp.log(row_mass)
    group_out = jnp.stack([row_target - row_top - log_mass, log_mass - row_spread / row_mass])
    all_out = lax.all_gather(group_out, "req", axis=1, tiled=True)

    offsets = dealt_offsets.reshape(-1)
    my_reqs = here * per_dev + jnp.arange(per_dev, dtype=jnp.int32)
    my_deal = jnp.take(deal_order, my_reqs)
    my_start = jnp.take(all_starts, my_reqs)
    my_len = jnp.take(all_lengths, my_reqs)
    pos = jnp.arange(slot_len, dtype=jnp.int32)[None, :]
    inside = (pos >= my_start[:, None]) & (pos < (my_start + my_len)[:, None])
    padded_out = jnp.pad(all_out, ((0, 0), (slot_len, slot_len)))
    out_at = (my_deal // per_dev) * CAP + jnp.take(offsets, my_deal) - my_start + slot_len
    picked = jax.vmap(lambda at: lax.dynamic_slice_in_dim(padded_out, at, slot_len, axis=1))(out_at)
    out_logprob = jnp.where(inside, picked[:, 0], 0.0)
    out_entropy = jnp.where(inside, picked[:, 1], 0.0)
    return (out_logprob, out_entropy)


def solution(mesh):
    in_specs = (
        P("req", None, None),
        P(),
        P("vocab", "req"),
        P("req", None),
        P("req"),
        P("req"),
        P(),
    )
    out_specs = (P("req", None), P("req", None))
    body = functools.partial(shards, mesh.shape["vocab"])
    return jax.shard_map(body, mesh=mesh, in_specs=in_specs, out_specs=out_specs, check_vma=False)
```

```python
import functools

import jax
import jax.numpy as jnp
from jax import lax
from jax.sharding import PartitionSpec as P

CAP = 224


eps = 1e-06


def compact_plan(row_base, lengths, capacity):
    offsets = jnp.cumsum(lengths) - lengths
    counter = jnp.arange(capacity, dtype=jnp.int32)
    member = jnp.sum((counter[:, None] >= offsets[None, :]).astype(jnp.int32), axis=1) - 1
    member_hot = (member[:, None] == jnp.arange(lengths.shape[0], dtype=jnp.int32)[None, :]).astype(
        jnp.int32
    )
    row_index = jnp.sum(member_hot * (row_base - offsets)[None, :], axis=1) + counter
    in_span = counter < jnp.sum(lengths)
    return (row_index, in_span)


def normalize(rows, gain):
    wide_rows = rows.astype(jnp.float32)
    scale = lax.rsqrt(jnp.mean(wide_rows * wide_rows, axis=-1, keepdims=True) + eps)
    return (wide_rows * scale * gain).astype(jnp.bfloat16)


def gather_by_all_to_all(x, axis, n):
    tiles = jnp.broadcast_to(x[None], (n,) + x.shape)
    return lax.all_to_all(tiles, axis, split_axis=0, concat_axis=0, tiled=True)


def shards(n_voc, hidden, gain, embedding, targets, span_start, span_len, deal_order):
    per_dev = hidden.shape[0]
    slot_len = hidden.shape[1]
    width = hidden.shape[2]
    total = deal_order.shape[0]
    n_req = total // per_dev
    voc_local = embedding.shape[0]
    piece = voc_local // n_req
    half = width // 2
    here = lax.axis_index("req")
    vhere = lax.axis_index("vocab")
    core = vhere % 2
    positions = jnp.arange(total, dtype=jnp.int32)
    source_of = jnp.sum(
        jnp.where(deal_order[None, :] == positions[:, None], positions[None, :], 0), axis=1
    )

    emb_piece = lax.all_to_all(embedding, "req", split_axis=0, concat_axis=1, tiled=True)

    meta = jnp.concatenate([targets, span_start[:, None], span_len[:, None]], axis=1)
    meta_all = gather_by_all_to_all(meta, "req", n_req).reshape(total, slot_len + 2)
    all_targets = meta_all[:, :slot_len]
    all_starts = meta_all[:, slot_len]
    all_lengths = meta_all[:, slot_len + 1]

    normed_home = normalize(hidden, gain)
    my_half = lax.dynamic_slice_in_dim(normed_home, core * half, half, axis=2)
    spread_rows = lax.all_to_all(my_half, "req", split_axis=1, concat_axis=0, tiled=True)
    dealt_rows = jnp.take(spread_rows, source_of, axis=0)
    home_rows = lax.all_to_all(dealt_rows, "req", split_axis=0, concat_axis=1, tiled=True)

    my_slots = here * per_dev + jnp.arange(per_dev, dtype=jnp.int32)
    members = jnp.take(source_of, my_slots)
    lengths = jnp.take(all_lengths, members)
    starts = jnp.take(all_starts, members)
    row_base = jnp.arange(per_dev, dtype=jnp.int32) * slot_len + starts
    row_index, in_span = compact_plan(row_base, lengths, CAP)
    safe_index = jnp.where(in_span, row_index, 0)
    compact_half = jnp.take(home_rows.reshape(per_dev * slot_len, half), safe_index, axis=0)

    rows_mine = lax.all_gather(compact_half, "req", axis=0, tiled=True)
    pairs = [(2 * k + j, 2 * k + 1 - j) for k in range(n_voc // 2) for j in range(2)]
    rows_other = lax.ppermute(rows_mine, "vocab", pairs)

    emb_mine = lax.dynamic_slice_in_dim(emb_piece, core * half, half, axis=1)
    emb_other = lax.dynamic_slice_in_dim(emb_piece, (1 - core) * half, half, axis=1)
    dims = (((1,), (1,)), ((), ()))
    logits = lax.dot_general(rows_mine, emb_mine, dims, preferred_element_type=jnp.float32)
    logits = logits + lax.dot_general(rows_other, emb_other, dims, preferred_element_type=jnp.float32)

    dealt_members = source_of.reshape(n_req, per_dev)
    dealt_lengths = jnp.take(all_lengths, dealt_members)
    dealt_offsets = jnp.cumsum(dealt_lengths, axis=1) - dealt_lengths
    dealt_starts = jnp.take(all_starts, dealt_members)
    member_targets = jnp.take(all_targets, source_of, axis=0).reshape(n_req, per_dev, slot_len)
    counter = jnp.arange(CAP, dtype=jnp.int32)
    source_pos = counter[None, None, :] - dealt_offsets[:, :, None] + dealt_starts[:, :, None]
    in_member = (counter[None, None, :] >= dealt_offsets[:, :, None]) & (
        counter[None, None, :] < (dealt_offsets + dealt_lengths)[:, :, None]
    )
    slot_ids = jnp.arange(slot_len, dtype=jnp.int32)
    hit = (source_pos[..., None] == slot_ids) & in_member[..., None]
    target_ids = jnp.sum(jnp.where(hit, member_targets[:, :, None, :], 0), axis=(1, 3)).reshape(-1)

    local_top = jnp.max(logits, axis=1)
    shifted = logits - local_top[:, None]
    weights = jnp.exp(shifted)
    local_mass = jnp.sum(weights, axis=1)
    local_spread = jnp.sum(weights * shifted, axis=1)
    local_ids = target_ids - (vhere * voc_local + here * piece)
    local_target = jnp.sum(
        jnp.where(jnp.arange(piece, dtype=jnp.int32)[None, :] == local_ids[:, None], logits, 0.0),
        axis=1,
    )

    def merge(stats):
        top_each, mass_each, spread_each, target_each = stats[:, 0], stats[:, 1], stats[:, 2], stats[:, 3]
        top = jnp.max(top_each, axis=0)
        gap = top_each - top[None, :]
        factor = jnp.exp(gap)
        mass = jnp.sum(factor * mass_each, axis=0)
        spread = jnp.sum(factor * (spread_each + gap * mass_each), axis=0)
        return jnp.stack([top, mass, spread, jnp.sum(target_each, axis=0)])

    local_stats = jnp.stack([local_top, local_mass, local_spread, local_target]).reshape(4, n_req, CAP)
    by_req = lax.all_to_all(local_stats.transpose(1, 0, 2), "req", split_axis=0, concat_axis=0, tiled=True)
    group_stats = merge(gather_by_all_to_all(merge(by_req), "vocab", n_voc))
    row_top, row_mass, row_spread, row_target = group_stats[0], group_stats[1], group_stats[2], group_stats[3]
    log_mass = jnp.log(row_mass)
    group_out = jnp.stack([row_target - row_top - log_mass, log_mass - row_spread / row_mass])
    all_out = gather_by_all_to_all(group_out, "req", n_req).transpose(1, 0, 2).reshape(2, n_req * CAP)

    offsets = dealt_offsets.reshape(-1)
    my_reqs = here * per_dev + jnp.arange(per_dev, dtype=jnp.int32)
    my_deal = jnp.take(deal_order, my_reqs)
    my_start = jnp.take(all_starts, my_reqs)
    my_len = jnp.take(all_lengths, my_reqs)
    pos = jnp.arange(slot_len, dtype=jnp.int32)[None, :]
    inside = (pos >= my_start[:, None]) & (pos < (my_start + my_len)[:, None])
    group_rows = jnp.take(all_out.reshape(2, n_req, CAP), my_deal // per_dev, axis=1)
    at = (jnp.take(offsets, my_deal) - my_start)[:, None] + pos
    pick = at[:, :, None] == jnp.arange(CAP, dtype=jnp.int32)
    picked = jnp.sum(jnp.where(pick[None], group_rows[:, :, None, :], 0.0), axis=3)
    out_logprob = jnp.where(inside, picked[0], 0.0)
    out_entropy = jnp.where(inside, picked[1], 0.0)
    return (out_logprob, out_entropy)


def solution(mesh):
    in_specs = (
        P("req", None, None),
        P(),
        P("vocab", "req"),
        P("req", None),
        P("req"),
        P("req"),
        P(),
    )
    out_specs = (P("req", None), P("req", None))
    body = functools.partial(shards, mesh.shape["vocab"])
    return jax.shard_map(body, mesh=mesh, in_specs=in_specs, out_specs=out_specs, check_vma=False)
```

```python
import functools

import jax
import jax.numpy as jnp
from jax import lax
from jax.sharding import PartitionSpec as P

CAP = 224


eps = 1e-06


def compact_plan(row_base, lengths, capacity):
    offsets = jnp.cumsum(lengths) - lengths
    counter = jnp.arange(capacity, dtype=jnp.int32)
    member = jnp.sum((counter[:, None] >= offsets[None, :]).astype(jnp.int32), axis=1) - 1
    member_hot = (member[:, None] == jnp.arange(lengths.shape[0], dtype=jnp.int32)[None, :]).astype(
        jnp.int32
    )
    row_index = jnp.sum(member_hot * (row_base - offsets)[None, :], axis=1) + counter
    in_span = counter < jnp.sum(lengths)
    return (row_index, in_span)


def normalize(rows, gain):
    wide_rows = rows.astype(jnp.float32)
    scale = lax.rsqrt(jnp.mean(wide_rows * wide_rows, axis=-1, keepdims=True) + eps)
    return (wide_rows * scale * gain).astype(jnp.bfloat16)


def gather_by_all_to_all(x, axis, n):
    tiles = jnp.broadcast_to(x[None], (n,) + x.shape)
    return lax.all_to_all(tiles, axis, split_axis=0, concat_axis=0, tiled=True)


def shards(n_voc, hidden, gain, embedding, targets, span_start, span_len, deal_order):
    per_dev = hidden.shape[0]
    slot_len = hidden.shape[1]
    width = hidden.shape[2]
    total = deal_order.shape[0]
    n_req = total // per_dev
    voc_local = embedding.shape[0]
    piece = voc_local // n_req
    half = width // 2
    here = lax.axis_index("req")
    vhere = lax.axis_index("vocab")
    core = vhere % 2
    positions = jnp.arange(total, dtype=jnp.int32)
    source_of = jnp.sum(
        jnp.where(deal_order[None, :] == positions[:, None], positions[None, :], 0), axis=1
    )

    normed_home = normalize(hidden, gain)
    my_half = lax.dynamic_slice_in_dim(normed_home, core * half, half, axis=2)
    block = slot_len // n_req
    hid_chunks = my_half.reshape(per_dev, n_req, block, half).transpose(1, 0, 2, 3).reshape(n_req, -1)
    emb_chunks = embedding.reshape(n_req, piece * embedding.shape[1])
    digits = jnp.stack([targets // 16384, (targets // 128) % 128, targets % 128], axis=1)
    bounds = jnp.zeros((per_dev, 1, slot_len), jnp.int32)
    bounds = bounds.at[:, 0, 0].set(span_start).at[:, 0, 1].set(span_len)
    meta = jnp.concatenate([digits, bounds], axis=1).astype(jnp.bfloat16).reshape(1, -1)
    meta_chunks = jnp.broadcast_to(meta, (n_req, meta.shape[1]))
    packed = jnp.concatenate([hid_chunks, emb_chunks, meta_chunks], axis=1)
    received = lax.all_to_all(packed, "req", split_axis=0, concat_axis=0, tiled=True)
    n_hid = hid_chunks.shape[1]
    n_emb = emb_chunks.shape[1]
    spread_rows = received[:, :n_hid].reshape(total, block, half)
    emb_piece = (
        received[:, n_hid : n_hid + n_emb]
        .reshape(n_req, piece, embedding.shape[1])
        .transpose(1, 0, 2)
        .reshape(piece, width)
    )
    meta_all = received[:, n_hid + n_emb :].astype(jnp.int32).reshape(total, 4, slot_len)
    all_targets = meta_all[:, 0] * 16384 + meta_all[:, 1] * 128 + meta_all[:, 2]
    all_starts = meta_all[:, 3, 0]
    all_lengths = meta_all[:, 3, 1]

    dealt_rows = jnp.take(spread_rows, source_of, axis=0)
    home_rows = lax.all_to_all(dealt_rows, "req", split_axis=0, concat_axis=1, tiled=True)

    my_slots = here * per_dev + jnp.arange(per_dev, dtype=jnp.int32)
    members = jnp.take(source_of, my_slots)
    lengths = jnp.take(all_lengths, members)
    starts = jnp.take(all_starts, members)
    row_base = jnp.arange(per_dev, dtype=jnp.int32) * slot_len + starts
    row_index, in_span = compact_plan(row_base, lengths, CAP)
    safe_index = jnp.where(in_span, row_index, 0)
    compact_half = jnp.take(home_rows.reshape(per_dev * slot_len, half), safe_index, axis=0)

    rows_mine = lax.all_gather(compact_half, "req", axis=0, tiled=True)
    pairs = [(2 * k + j, 2 * k + 1 - j) for k in range(n_voc // 2) for j in range(2)]
    rows_other = lax.ppermute(rows_mine, "vocab", pairs)

    emb_mine = lax.dynamic_slice_in_dim(emb_piece, core * half, half, axis=1)
    emb_other = lax.dynamic_slice_in_dim(emb_piece, (1 - core) * half, half, axis=1)
    dims = (((1,), (1,)), ((), ()))
    logits = lax.dot_general(rows_mine, emb_mine, dims, preferred_element_type=jnp.float32)
    logits = logits + lax.dot_general(rows_other, emb_other, dims, preferred_element_type=jnp.float32)

    dealt_members = source_of.reshape(n_req, per_dev)
    dealt_lengths = jnp.take(all_lengths, dealt_members)
    dealt_offsets = jnp.cumsum(dealt_lengths, axis=1) - dealt_lengths
    dealt_starts = jnp.take(all_starts, dealt_members)
    member_targets = jnp.take(all_targets, source_of, axis=0).reshape(n_req, per_dev, slot_len)
    counter = jnp.arange(CAP, dtype=jnp.int32)
    source_pos = counter[None, None, :] - dealt_offsets[:, :, None] + dealt_starts[:, :, None]
    in_member = (counter[None, None, :] >= dealt_offsets[:, :, None]) & (
        counter[None, None, :] < (dealt_offsets + dealt_lengths)[:, :, None]
    )
    slot_ids = jnp.arange(slot_len, dtype=jnp.int32)
    hit = (source_pos[..., None] == slot_ids) & in_member[..., None]
    target_ids = jnp.sum(jnp.where(hit, member_targets[:, :, None, :], 0), axis=(1, 3)).reshape(-1)

    local_top = jnp.max(logits, axis=1)
    shifted = logits - local_top[:, None]
    weights = jnp.exp(shifted)
    local_mass = jnp.sum(weights, axis=1)
    local_spread = jnp.sum(weights * shifted, axis=1)
    local_ids = target_ids - (vhere * voc_local + here * piece)
    local_target = jnp.sum(
        jnp.where(jnp.arange(piece, dtype=jnp.int32)[None, :] == local_ids[:, None], logits, 0.0),
        axis=1,
    )

    def merge(stats):
        top_each, mass_each, spread_each, target_each = stats[:, 0], stats[:, 1], stats[:, 2], stats[:, 3]
        top = jnp.max(top_each, axis=0)
        gap = top_each - top[None, :]
        factor = jnp.exp(gap)
        mass = jnp.sum(factor * mass_each, axis=0)
        spread = jnp.sum(factor * (spread_each + gap * mass_each), axis=0)
        return jnp.stack([top, mass, spread, jnp.sum(target_each, axis=0)])

    local_stats = jnp.stack([local_top, local_mass, local_spread, local_target]).reshape(4, n_req, CAP)
    by_req = lax.all_to_all(local_stats.transpose(1, 0, 2), "req", split_axis=0, concat_axis=0, tiled=True)
    group_stats = merge(gather_by_all_to_all(merge(by_req), "vocab", n_voc))
    row_top, row_mass, row_spread, row_target = group_stats[0], group_stats[1], group_stats[2], group_stats[3]
    log_mass = jnp.log(row_mass)
    group_out = jnp.stack([row_target - row_top - log_mass, log_mass - row_spread / row_mass])
    all_out = gather_by_all_to_all(group_out, "req", n_req).transpose(1, 0, 2).reshape(2, n_req * CAP)

    offsets = dealt_offsets.reshape(-1)
    my_reqs = here * per_dev + jnp.arange(per_dev, dtype=jnp.int32)
    my_deal = jnp.take(deal_order, my_reqs)
    my_start = jnp.take(all_starts, my_reqs)
    my_len = jnp.take(all_lengths, my_reqs)
    pos = jnp.arange(slot_len, dtype=jnp.int32)[None, :]
    inside = (pos >= my_start[:, None]) & (pos < (my_start + my_len)[:, None])
    group_rows = jnp.take(all_out.reshape(2, n_req, CAP), my_deal // per_dev, axis=1)
    at = (jnp.take(offsets, my_deal) - my_start)[:, None] + pos
    pick = at[:, :, None] == jnp.arange(CAP, dtype=jnp.int32)
    picked = jnp.sum(jnp.where(pick[None], group_rows[:, :, None, :], 0.0), axis=3)
    out_logprob = jnp.where(inside, picked[0], 0.0)
    out_entropy = jnp.where(inside, picked[1], 0.0)
    return (out_logprob, out_entropy)


def solution(mesh):
    in_specs = (
        P("req", None, None),
        P(),
        P("vocab", "req"),
        P("req", None),
        P("req"),
        P("req"),
        P(),
    )
    out_specs = (P("req", None), P("req", None))
    body = functools.partial(shards, mesh.shape["vocab"])
    return jax.shard_map(body, mesh=mesh, in_specs=in_specs, out_specs=out_specs, check_vma=False)
```

```python
import functools

import jax
import jax.numpy as jnp
from jax import lax
from jax.sharding import PartitionSpec as P

CAP = 224


eps = 1e-06


def compact_plan(row_base, lengths, capacity):
    offsets = jnp.cumsum(lengths) - lengths
    counter = jnp.arange(capacity, dtype=jnp.int32)
    member = jnp.sum((counter[:, None] >= offsets[None, :]).astype(jnp.int32), axis=1) - 1
    member_hot = (member[:, None] == jnp.arange(lengths.shape[0], dtype=jnp.int32)[None, :]).astype(
        jnp.int32
    )
    row_index = jnp.sum(member_hot * (row_base - offsets)[None, :], axis=1) + counter
    in_span = counter < jnp.sum(lengths)
    return (row_index, in_span)


def normalize(rows, gain):
    wide_rows = rows.astype(jnp.float32)
    scale = lax.rsqrt(jnp.mean(wide_rows * wide_rows, axis=-1, keepdims=True) + eps)
    return (wide_rows * scale * gain).astype(jnp.bfloat16)


def gather_by_all_to_all(x, axis, n):
    tiles = jnp.broadcast_to(x[None], (n,) + x.shape)
    return lax.all_to_all(tiles, axis, split_axis=0, concat_axis=0, tiled=True)


def shards(n_voc, hidden, gain, embedding, targets, span_start, span_len, deal_order):
    per_dev = hidden.shape[0]
    slot_len = hidden.shape[1]
    width = hidden.shape[2]
    total = deal_order.shape[0]
    n_req = total // per_dev
    voc_local = embedding.shape[0]
    piece = voc_local // n_req
    half = width // 2
    here = lax.axis_index("req")
    vhere = lax.axis_index("vocab")
    core = vhere % 2
    positions = jnp.arange(total, dtype=jnp.int32)
    source_of = jnp.sum(
        jnp.where(deal_order[None, :] == positions[:, None], positions[None, :], 0), axis=1
    )

    emb_piece = lax.all_to_all(embedding, "req", split_axis=0, concat_axis=1, tiled=True)

    normed_home = normalize(hidden, gain)
    my_half = lax.dynamic_slice_in_dim(normed_home, core * half, half, axis=2)
    block = slot_len // n_req
    digits = jnp.stack([targets // 16384, (targets // 128) % 128, targets % 128], axis=1)
    bounds = jnp.zeros((per_dev, 1, slot_len), jnp.int32)
    bounds = bounds.at[:, 0, 0].set(span_start).at[:, 0, 1].set(span_len)
    meta = jnp.concatenate([digits, bounds], axis=1).astype(jnp.bfloat16).reshape(per_dev, 1, 1, -1)
    meta = jnp.pad(meta, ((0, 0), (0, 0), (0, 0), (0, half - meta.shape[3])))
    blocks = jnp.concatenate(
        [my_half.reshape(per_dev, n_req, block, half), jnp.broadcast_to(meta, (per_dev, n_req, 1, half))],
        axis=2,
    ).reshape(per_dev, n_req * (block + 1), half)
    received = lax.all_to_all(blocks, "req", split_axis=1, concat_axis=0, tiled=True)
    spread_rows = received[:, :block]
    meta_all = received[:, block, : 4 * slot_len].astype(jnp.int32).reshape(total, 4, slot_len)
    all_targets = meta_all[:, 0] * 16384 + meta_all[:, 1] * 128 + meta_all[:, 2]
    all_starts = meta_all[:, 3, 0]
    all_lengths = meta_all[:, 3, 1]
    dealt_rows = jnp.take(spread_rows, source_of, axis=0)
    home_rows = lax.all_to_all(dealt_rows, "req", split_axis=0, concat_axis=1, tiled=True)

    my_slots = here * per_dev + jnp.arange(per_dev, dtype=jnp.int32)
    members = jnp.take(source_of, my_slots)
    lengths = jnp.take(all_lengths, members)
    starts = jnp.take(all_starts, members)
    row_base = jnp.arange(per_dev, dtype=jnp.int32) * slot_len + starts
    row_index, in_span = compact_plan(row_base, lengths, CAP)
    safe_index = jnp.where(in_span, row_index, 0)
    compact_half = jnp.take(home_rows.reshape(per_dev * slot_len, half), safe_index, axis=0)

    rows_mine = lax.all_gather(compact_half, "req", axis=0, tiled=True)
    pairs = [(2 * k + j, 2 * k + 1 - j) for k in range(n_voc // 2) for j in range(2)]
    rows_other = lax.ppermute(rows_mine, "vocab", pairs)

    emb_mine = lax.dynamic_slice_in_dim(emb_piece, core * half, half, axis=1)
    emb_other = lax.dynamic_slice_in_dim(emb_piece, (1 - core) * half, half, axis=1)
    dims = (((1,), (1,)), ((), ()))
    logits = lax.dot_general(rows_mine, emb_mine, dims, preferred_element_type=jnp.float32)
    logits = logits + lax.dot_general(rows_other, emb_other, dims, preferred_element_type=jnp.float32)

    dealt_members = source_of.reshape(n_req, per_dev)
    dealt_lengths = jnp.take(all_lengths, dealt_members)
    dealt_offsets = jnp.cumsum(dealt_lengths, axis=1) - dealt_lengths
    dealt_starts = jnp.take(all_starts, dealt_members)
    member_targets = jnp.take(all_targets, source_of, axis=0).reshape(n_req, per_dev, slot_len)
    counter = jnp.arange(CAP, dtype=jnp.int32)
    source_pos = counter[None, None, :] - dealt_offsets[:, :, None] + dealt_starts[:, :, None]
    in_member = (counter[None, None, :] >= dealt_offsets[:, :, None]) & (
        counter[None, None, :] < (dealt_offsets + dealt_lengths)[:, :, None]
    )
    slot_ids = jnp.arange(slot_len, dtype=jnp.int32)
    hit = (source_pos[..., None] == slot_ids) & in_member[..., None]
    target_ids = jnp.sum(jnp.where(hit, member_targets[:, :, None, :], 0), axis=(1, 3)).reshape(-1)

    local_top = jnp.max(logits, axis=1)
    shifted = logits - local_top[:, None]
    weights = jnp.exp(shifted)
    local_mass = jnp.sum(weights, axis=1)
    local_spread = jnp.sum(weights * shifted, axis=1)
    local_ids = target_ids - (vhere * voc_local + here * piece)
    local_target = jnp.sum(
        jnp.where(jnp.arange(piece, dtype=jnp.int32)[None, :] == local_ids[:, None], logits, 0.0),
        axis=1,
    )

    def merge(stats):
        top_each, mass_each, spread_each, target_each = stats[:, 0], stats[:, 1], stats[:, 2], stats[:, 3]
        top = jnp.max(top_each, axis=0)
        gap = top_each - top[None]
        factor = jnp.exp(gap)
        mass = jnp.sum(factor * mass_each, axis=0)
        spread = jnp.sum(factor * (spread_each + gap * mass_each), axis=0)
        return jnp.stack([top, mass, spread, jnp.sum(target_each, axis=0)])

    offsets = dealt_offsets.reshape(-1)
    pos = jnp.arange(slot_len, dtype=jnp.int32)[None, :]
    local_stats = jnp.stack([local_top, local_mass, local_spread, local_target]).reshape(4, n_req, CAP)
    request_rows = jnp.take(local_stats, deal_order // per_dev, axis=1)
    at = (jnp.take(offsets, deal_order) - all_starts)[:, None] + pos
    pick = at[:, :, None] == jnp.arange(CAP, dtype=jnp.int32)
    picked = jnp.sum(jnp.where(pick[None], request_rows[:, :, None, :], 0.0), axis=3)
    to_home = picked.reshape(4, n_req, per_dev, slot_len).transpose(1, 0, 2, 3)
    by_req = merge(lax.all_to_all(to_home, "req", split_axis=0, concat_axis=0, tiled=True))
    row_top, row_mass, row_spread, row_target = merge(gather_by_all_to_all(by_req, "vocab", n_voc))
    log_mass = jnp.log(row_mass)

    my_reqs = here * per_dev + jnp.arange(per_dev, dtype=jnp.int32)
    my_start = jnp.take(all_starts, my_reqs)
    my_len = jnp.take(all_lengths, my_reqs)
    inside = (pos >= my_start[:, None]) & (pos < (my_start + my_len)[:, None])
    out_logprob = jnp.where(inside, row_target - row_top - log_mass, 0.0)
    out_entropy = jnp.where(inside, log_mass - row_spread / row_mass, 0.0)
    return (out_logprob, out_entropy)


def solution(mesh):
    in_specs = (
        P("req", None, None),
        P(),
        P("vocab", "req"),
        P("req", None),
        P("req"),
        P("req"),
        P(),
    )
    out_specs = (P("req", None), P("req", None))
    body = functools.partial(shards, mesh.shape["vocab"])
    return jax.shard_map(body, mesh=mesh, in_specs=in_specs, out_specs=out_specs, check_vma=False)
```

```python
import functools

import jax
import jax.numpy as jnp
from jax import lax
from jax.sharding import PartitionSpec as P

CAP = 224


eps = 1e-06


def compact_plan(row_base, lengths, capacity):
    offsets = jnp.cumsum(lengths) - lengths
    counter = jnp.arange(capacity, dtype=jnp.int32)
    member = jnp.sum((counter[:, None] >= offsets[None, :]).astype(jnp.int32), axis=1) - 1
    member_hot = (member[:, None] == jnp.arange(lengths.shape[0], dtype=jnp.int32)[None, :]).astype(
        jnp.int32
    )
    row_index = jnp.sum(member_hot * (row_base - offsets)[None, :], axis=1) + counter
    in_span = counter < jnp.sum(lengths)
    return (row_index, in_span)


def normalize(rows, gain):
    wide_rows = rows.astype(jnp.float32)
    scale = lax.rsqrt(jnp.mean(wide_rows * wide_rows, axis=-1, keepdims=True) + eps)
    return (wide_rows * scale * gain).astype(jnp.bfloat16)


def gather_by_all_to_all(x, axis, n):
    tiles = jnp.broadcast_to(x[None], (n,) + x.shape)
    return lax.all_to_all(tiles, axis, split_axis=0, concat_axis=0, tiled=True)


def shards(n_voc, hidden, gain, embedding, targets, span_start, span_len, deal_order):
    per_dev = hidden.shape[0]
    slot_len = hidden.shape[1]
    width = hidden.shape[2]
    total = deal_order.shape[0]
    n_req = total // per_dev
    voc_local = embedding.shape[0]
    piece = voc_local // n_req
    half = width // 2
    here = lax.axis_index("req")
    vhere = lax.axis_index("vocab")
    core = vhere % 2
    positions = jnp.arange(total, dtype=jnp.int32)
    source_of = jnp.sum(
        jnp.where(deal_order[None, :] == positions[:, None], positions[None, :], 0), axis=1
    )

    emb_chunks = embedding.reshape(n_req, piece, embedding.shape[1])
    by_source = [lax.dynamic_index_in_dim(emb_chunks, here, keepdims=False)]
    for shift in range(1, n_req):
        outgoing = lax.dynamic_index_in_dim(emb_chunks, (here + shift) % n_req, keepdims=False)
        perm = [(i, (i + shift) % n_req) for i in range(n_req)]
        by_source.append(lax.ppermute(outgoing, "req", perm))
    stacked = jnp.stack(by_source)
    order = (here - jnp.arange(n_req, dtype=jnp.int32)) % n_req
    emb_piece = (
        jnp.zeros_like(stacked).at[order].set(stacked).transpose(1, 0, 2).reshape(piece, width)
    )

    normed_home = normalize(hidden, gain)
    my_half = lax.dynamic_slice_in_dim(normed_home, core * half, half, axis=2)
    block = slot_len // n_req
    digits = jnp.stack([targets // 16384, (targets // 128) % 128, targets % 128], axis=1)
    bounds = jnp.zeros((per_dev, 1, slot_len), jnp.int32)
    bounds = bounds.at[:, 0, 0].set(span_start).at[:, 0, 1].set(span_len)
    meta = jnp.concatenate([digits, bounds], axis=1).astype(jnp.bfloat16).reshape(per_dev, 1, 1, -1)
    meta = jnp.pad(meta, ((0, 0), (0, 0), (0, 0), (0, half - meta.shape[3])))
    blocks = jnp.concatenate(
        [my_half.reshape(per_dev, n_req, block, half), jnp.broadcast_to(meta, (per_dev, n_req, 1, half))],
        axis=2,
    ).reshape(per_dev, n_req * (block + 1), half)
    received = lax.all_to_all(blocks, "req", split_axis=1, concat_axis=0, tiled=True)
    spread_rows = received[:, :block]
    meta_all = received[:, block, : 4 * slot_len].astype(jnp.int32).reshape(total, 4, slot_len)
    all_targets = meta_all[:, 0] * 16384 + meta_all[:, 1] * 128 + meta_all[:, 2]
    all_starts = meta_all[:, 3, 0]
    all_lengths = meta_all[:, 3, 1]
    dealt_rows = jnp.take(spread_rows, source_of, axis=0)
    home_rows = lax.all_to_all(dealt_rows, "req", split_axis=0, concat_axis=1, tiled=True)

    my_slots = here * per_dev + jnp.arange(per_dev, dtype=jnp.int32)
    members = jnp.take(source_of, my_slots)
    lengths = jnp.take(all_lengths, members)
    starts = jnp.take(all_starts, members)
    row_base = jnp.arange(per_dev, dtype=jnp.int32) * slot_len + starts
    row_index, in_span = compact_plan(row_base, lengths, CAP)
    safe_index = jnp.where(in_span, row_index, 0)
    compact_half = jnp.take(home_rows.reshape(per_dev * slot_len, half), safe_index, axis=0)

    rows_mine = lax.all_gather(compact_half, "req", axis=0, tiled=True)
    pairs = [(2 * k + j, 2 * k + 1 - j) for k in range(n_voc // 2) for j in range(2)]
    rows_other = lax.ppermute(rows_mine, "vocab", pairs)

    emb_mine = lax.dynamic_slice_in_dim(emb_piece, core * half, half, axis=1)
    emb_other = lax.dynamic_slice_in_dim(emb_piece, (1 - core) * half, half, axis=1)
    dims = (((1,), (1,)), ((), ()))
    logits = lax.dot_general(rows_mine, emb_mine, dims, preferred_element_type=jnp.float32)
    logits = logits + lax.dot_general(rows_other, emb_other, dims, preferred_element_type=jnp.float32)

    dealt_members = source_of.reshape(n_req, per_dev)
    dealt_lengths = jnp.take(all_lengths, dealt_members)
    dealt_offsets = jnp.cumsum(dealt_lengths, axis=1) - dealt_lengths
    dealt_starts = jnp.take(all_starts, dealt_members)
    member_targets = jnp.take(all_targets, source_of, axis=0).reshape(n_req, per_dev, slot_len)
    counter = jnp.arange(CAP, dtype=jnp.int32)
    source_pos = counter[None, None, :] - dealt_offsets[:, :, None] + dealt_starts[:, :, None]
    in_member = (counter[None, None, :] >= dealt_offsets[:, :, None]) & (
        counter[None, None, :] < (dealt_offsets + dealt_lengths)[:, :, None]
    )
    slot_ids = jnp.arange(slot_len, dtype=jnp.int32)
    hit = (source_pos[..., None] == slot_ids) & in_member[..., None]
    target_ids = jnp.sum(jnp.where(hit, member_targets[:, :, None, :], 0), axis=(1, 3)).reshape(-1)

    local_top = jnp.max(logits, axis=1)
    shifted = logits - local_top[:, None]
    weights = jnp.exp(shifted)
    local_mass = jnp.sum(weights, axis=1)
    local_spread = jnp.sum(weights * shifted, axis=1)
    local_ids = target_ids - (vhere * voc_local + here * piece)
    local_target = jnp.sum(
        jnp.where(jnp.arange(piece, dtype=jnp.int32)[None, :] == local_ids[:, None], logits, 0.0),
        axis=1,
    )

    def merge(stats):
        top_each, mass_each, spread_each, target_each = stats[:, 0], stats[:, 1], stats[:, 2], stats[:, 3]
        top = jnp.max(top_each, axis=0)
        gap = top_each - top[None]
        factor = jnp.exp(gap)
        mass = jnp.sum(factor * mass_each, axis=0)
        spread = jnp.sum(factor * (spread_each + gap * mass_each), axis=0)
        return jnp.stack([top, mass, spread, jnp.sum(target_each, axis=0)])

    offsets = dealt_offsets.reshape(-1)
    pos = jnp.arange(slot_len, dtype=jnp.int32)[None, :]
    local_stats = jnp.stack([local_top, local_mass, local_spread, local_target]).reshape(4, n_req, CAP)
    request_rows = jnp.take(local_stats, deal_order // per_dev, axis=1)
    at = (jnp.take(offsets, deal_order) - all_starts)[:, None] + pos
    pick = at[:, :, None] == jnp.arange(CAP, dtype=jnp.int32)
    picked = jnp.sum(jnp.where(pick[None], request_rows[:, :, None, :], 0.0), axis=3)
    to_home = picked.reshape(4, n_req, per_dev, slot_len).transpose(1, 0, 2, 3)
    by_req = merge(lax.all_to_all(to_home, "req", split_axis=0, concat_axis=0, tiled=True))
    row_top, row_mass, row_spread, row_target = merge(gather_by_all_to_all(by_req, "vocab", n_voc))
    log_mass = jnp.log(row_mass)

    my_reqs = here * per_dev + jnp.arange(per_dev, dtype=jnp.int32)
    my_start = jnp.take(all_starts, my_reqs)
    my_len = jnp.take(all_lengths, my_reqs)
    inside = (pos >= my_start[:, None]) & (pos < (my_start + my_len)[:, None])
    out_logprob = jnp.where(inside, row_target - row_top - log_mass, 0.0)
    out_entropy = jnp.where(inside, log_mass - row_spread / row_mass, 0.0)
    return (out_logprob, out_entropy)


def solution(mesh):
    in_specs = (
        P("req", None, None),
        P(),
        P("vocab", "req"),
        P("req", None),
        P("req"),
        P("req"),
        P(),
    )
    out_specs = (P("req", None), P("req", None))
    body = functools.partial(shards, mesh.shape["vocab"])
    return jax.shard_map(body, mesh=mesh, in_specs=in_specs, out_specs=out_specs, check_vma=False)
```

```python
import functools

import jax
import jax.numpy as jnp
from jax import lax
from jax.sharding import PartitionSpec as P

CAP = 224


eps = 1e-06


def compact_plan(row_base, lengths, capacity):
    offsets = jnp.cumsum(lengths) - lengths
    counter = jnp.arange(capacity, dtype=jnp.int32)
    member = jnp.sum((counter[:, None] >= offsets[None, :]).astype(jnp.int32), axis=1) - 1
    member_hot = (member[:, None] == jnp.arange(lengths.shape[0], dtype=jnp.int32)[None, :]).astype(
        jnp.int32
    )
    row_index = jnp.sum(member_hot * (row_base - offsets)[None, :], axis=1) + counter
    in_span = counter < jnp.sum(lengths)
    return (row_index, in_span)


def normalize(rows, gain):
    wide_rows = rows.astype(jnp.float32)
    scale = lax.rsqrt(jnp.mean(wide_rows * wide_rows, axis=-1, keepdims=True) + eps)
    return (wide_rows * scale * gain).astype(jnp.bfloat16)


def gather_by_all_to_all(x, axis, n):
    tiles = jnp.broadcast_to(x[None], (n,) + x.shape)
    return lax.all_to_all(tiles, axis, split_axis=0, concat_axis=0, tiled=True)


def shards(n_voc, hidden, gain, embedding, targets, span_start, span_len, deal_order):
    per_dev = hidden.shape[0]
    slot_len = hidden.shape[1]
    width = hidden.shape[2]
    total = deal_order.shape[0]
    n_req = total // per_dev
    voc_local = embedding.shape[0]
    piece = voc_local // n_req
    half = width // 2
    here = lax.axis_index("req")
    vhere = lax.axis_index("vocab")
    core = vhere % 2
    positions = jnp.arange(total, dtype=jnp.int32)
    source_of = jnp.sum(
        jnp.where(deal_order[None, :] == positions[:, None], positions[None, :], 0), axis=1
    )

    emb_blocks = lax.all_to_all(embedding, "req", split_axis=0, concat_axis=0, tiled=True)
    emb_piece = emb_blocks.reshape(n_req, piece, -1).transpose(1, 0, 2).reshape(piece, width)

    normed_home = normalize(hidden, gain)
    my_half = lax.dynamic_slice_in_dim(normed_home, core * half, half, axis=2)
    block = slot_len // n_req
    digits = jnp.stack([targets // 16384, (targets // 128) % 128, targets % 128], axis=1)
    bounds = jnp.zeros((per_dev, 1, slot_len), jnp.int32)
    bounds = bounds.at[:, 0, 0].set(span_start).at[:, 0, 1].set(span_len)
    meta = jnp.concatenate([digits, bounds], axis=1).astype(jnp.bfloat16).reshape(per_dev, 1, 1, -1)
    meta = jnp.pad(meta, ((0, 0), (0, 0), (0, 0), (0, half - meta.shape[3])))
    blocks = jnp.concatenate(
        [my_half.reshape(per_dev, n_req, block, half), jnp.broadcast_to(meta, (per_dev, n_req, 1, half))],
        axis=2,
    ).reshape(per_dev, n_req * (block + 1), half)
    received = lax.all_to_all(blocks, "req", split_axis=1, concat_axis=0, tiled=True)
    spread_rows = received[:, :block]
    meta_all = received[:, block, : 4 * slot_len].astype(jnp.int32).reshape(total, 4, slot_len)
    all_targets = meta_all[:, 0] * 16384 + meta_all[:, 1] * 128 + meta_all[:, 2]
    all_starts = meta_all[:, 3, 0]
    all_lengths = meta_all[:, 3, 1]
    dealt_rows = jnp.take(spread_rows, source_of, axis=0)
    home_rows = lax.all_to_all(dealt_rows, "req", split_axis=0, concat_axis=0, tiled=True)

    my_slots = here * per_dev + jnp.arange(per_dev, dtype=jnp.int32)
    members = jnp.take(source_of, my_slots)
    lengths = jnp.take(all_lengths, members)
    starts = jnp.take(all_starts, members)
    row_base = jnp.arange(per_dev, dtype=jnp.int32) * slot_len + starts
    row_index, in_span = compact_plan(row_base, lengths, CAP)
    safe_index = jnp.where(in_span, row_index, 0)
    request, position = safe_index // slot_len, safe_index % slot_len
    block_index = (position // block) * (per_dev * block) + request * block + position % block
    compact_half = jnp.take(home_rows.reshape(per_dev * slot_len, half), block_index, axis=0)

    rows_mine = lax.all_gather(compact_half, "req", axis=0, tiled=True)
    pairs = [(2 * k + j, 2 * k + 1 - j) for k in range(n_voc // 2) for j in range(2)]
    rows_other = lax.ppermute(rows_mine, "vocab", pairs)

    emb_mine = lax.dynamic_slice_in_dim(emb_piece, core * half, half, axis=1)
    emb_other = lax.dynamic_slice_in_dim(emb_piece, (1 - core) * half, half, axis=1)
    dims = (((1,), (1,)), ((), ()))
    logits = lax.dot_general(rows_mine, emb_mine, dims, preferred_element_type=jnp.float32)
    logits = logits + lax.dot_general(rows_other, emb_other, dims, preferred_element_type=jnp.float32)

    dealt_members = source_of.reshape(n_req, per_dev)
    dealt_lengths = jnp.take(all_lengths, dealt_members)
    dealt_offsets = jnp.cumsum(dealt_lengths, axis=1) - dealt_lengths
    dealt_starts = jnp.take(all_starts, dealt_members)
    member_targets = jnp.take(all_targets, source_of, axis=0).reshape(n_req, per_dev, slot_len)
    counter = jnp.arange(CAP, dtype=jnp.int32)
    source_pos = counter[None, None, :] - dealt_offsets[:, :, None] + dealt_starts[:, :, None]
    in_member = (counter[None, None, :] >= dealt_offsets[:, :, None]) & (
        counter[None, None, :] < (dealt_offsets + dealt_lengths)[:, :, None]
    )
    slot_ids = jnp.arange(slot_len, dtype=jnp.int32)
    hit = (source_pos[..., None] == slot_ids) & in_member[..., None]
    target_ids = jnp.sum(jnp.where(hit, member_targets[:, :, None, :], 0), axis=(1, 3)).reshape(-1)

    local_top = jnp.max(logits, axis=1)
    shifted = logits - local_top[:, None]
    weights = jnp.exp(shifted)
    local_mass = jnp.sum(weights, axis=1)
    local_spread = jnp.sum(weights * shifted, axis=1)
    local_ids = target_ids - (vhere * voc_local + here * piece)
    local_target = jnp.sum(
        jnp.where(jnp.arange(piece, dtype=jnp.int32)[None, :] == local_ids[:, None], logits, 0.0),
        axis=1,
    )

    def merge(stats):
        top_each, mass_each, spread_each, target_each = stats[:, 0], stats[:, 1], stats[:, 2], stats[:, 3]
        top = jnp.max(top_each, axis=0)
        gap = top_each - top[None]
        factor = jnp.exp(gap)
        mass = jnp.sum(factor * mass_each, axis=0)
        spread = jnp.sum(factor * (spread_each + gap * mass_each), axis=0)
        return jnp.stack([top, mass, spread, jnp.sum(target_each, axis=0)])

    offsets = dealt_offsets.reshape(-1)
    pos = jnp.arange(slot_len, dtype=jnp.int32)[None, :]
    local_stats = jnp.stack([local_top, local_mass, local_spread, local_target]).reshape(4, n_req, CAP)
    request_rows = jnp.take(local_stats, deal_order // per_dev, axis=1)
    at = (jnp.take(offsets, deal_order) - all_starts)[:, None] + pos
    pick = at[:, :, None] == jnp.arange(CAP, dtype=jnp.int32)
    picked = jnp.sum(jnp.where(pick[None], request_rows[:, :, None, :], 0.0), axis=3)
    to_home = picked.reshape(4, n_req, per_dev, slot_len).transpose(1, 0, 2, 3)
    by_req = merge(lax.all_to_all(to_home, "req", split_axis=0, concat_axis=0, tiled=True))
    row_top, row_mass, row_spread, row_target = merge(gather_by_all_to_all(by_req, "vocab", n_voc))
    log_mass = jnp.log(row_mass)

    my_reqs = here * per_dev + jnp.arange(per_dev, dtype=jnp.int32)
    my_start = jnp.take(all_starts, my_reqs)
    my_len = jnp.take(all_lengths, my_reqs)
    inside = (pos >= my_start[:, None]) & (pos < (my_start + my_len)[:, None])
    out_logprob = jnp.where(inside, row_target - row_top - log_mass, 0.0)
    out_entropy = jnp.where(inside, log_mass - row_spread / row_mass, 0.0)
    return (out_logprob, out_entropy)


def solution(mesh):
    in_specs = (
        P("req", None, None),
        P(),
        P("vocab", "req"),
        P("req", None),
        P("req"),
        P("req"),
        P(),
    )
    out_specs = (P("req", None), P("req", None))
    body = functools.partial(shards, mesh.shape["vocab"])
    return jax.shard_map(body, mesh=mesh, in_specs=in_specs, out_specs=out_specs, check_vma=False)
```

```python
import functools

import jax
import jax.numpy as jnp
from jax import lax
from jax.sharding import PartitionSpec as P

CAP = 224


eps = 1e-06


def compact_plan(row_base, lengths, capacity):
    offsets = jnp.cumsum(lengths) - lengths
    counter = jnp.arange(capacity, dtype=jnp.int32)
    member = jnp.sum((counter[:, None] >= offsets[None, :]).astype(jnp.int32), axis=1) - 1
    member_hot = (member[:, None] == jnp.arange(lengths.shape[0], dtype=jnp.int32)[None, :]).astype(
        jnp.int32
    )
    row_index = jnp.sum(member_hot * (row_base - offsets)[None, :], axis=1) + counter
    in_span = counter < jnp.sum(lengths)
    return (row_index, in_span)


def normalize(rows, gain):
    wide_rows = rows.astype(jnp.float32)
    scale = lax.rsqrt(jnp.mean(wide_rows * wide_rows, axis=-1, keepdims=True) + eps)
    return (wide_rows * scale * gain).astype(jnp.bfloat16)


def gather_by_all_to_all(x, axis, n):
    tiles = jnp.broadcast_to(x[None], (n,) + x.shape)
    return lax.all_to_all(tiles, axis, split_axis=0, concat_axis=0, tiled=True)


def shards(n_voc, hidden, gain, embedding, targets, span_start, span_len, deal_order):
    per_dev = hidden.shape[0]
    slot_len = hidden.shape[1]
    width = hidden.shape[2]
    total = deal_order.shape[0]
    n_req = total // per_dev
    voc_local = embedding.shape[0]
    piece = voc_local // n_req
    half = width // 2
    here = lax.axis_index("req")
    vhere = lax.axis_index("vocab")
    core = vhere % 2
    positions = jnp.arange(total, dtype=jnp.int32)
    source_of = jnp.sum(
        jnp.where(deal_order[None, :] == positions[:, None], positions[None, :], 0), axis=1
    )

    emb_piece = lax.all_to_all(embedding, "req", split_axis=0, concat_axis=1, tiled=True)

    normed_home = normalize(hidden, gain)
    my_half = lax.dynamic_slice_in_dim(normed_home, core * half, half, axis=2)
    block = slot_len // n_req
    digits = jnp.stack([targets // 16384, (targets // 128) % 128, targets % 128], axis=1)
    bounds = jnp.zeros((per_dev, 1, slot_len), jnp.int32)
    bounds = bounds.at[:, 0, 0].set(span_start).at[:, 0, 1].set(span_len)
    meta = jnp.concatenate([digits, bounds], axis=1).astype(jnp.bfloat16).reshape(per_dev, 1, 1, -1)
    meta = jnp.pad(meta, ((0, 0), (0, 0), (0, 0), (0, half - meta.shape[3])))
    blocks = jnp.concatenate(
        [my_half.reshape(per_dev, n_req, block, half), jnp.broadcast_to(meta, (per_dev, n_req, 1, half))],
        axis=2,
    ).transpose(1, 0, 2, 3)
    received = lax.all_to_all(blocks, "req", split_axis=0, concat_axis=0, tiled=True)
    spread_rows = received[:, :, :block].reshape(total, block, half)
    meta_all = received[:, :, block, : 4 * slot_len].astype(jnp.int32).reshape(total, 4, slot_len)
    all_targets = meta_all[:, 0] * 16384 + meta_all[:, 1] * 128 + meta_all[:, 2]
    all_starts = meta_all[:, 3, 0]
    all_lengths = meta_all[:, 3, 1]
    dealt_rows = jnp.take(spread_rows, source_of, axis=0)
    home_rows = lax.all_to_all(dealt_rows, "req", split_axis=0, concat_axis=1, tiled=True)

    my_slots = here * per_dev + jnp.arange(per_dev, dtype=jnp.int32)
    members = jnp.take(source_of, my_slots)
    lengths = jnp.take(all_lengths, members)
    starts = jnp.take(all_starts, members)
    row_base = jnp.arange(per_dev, dtype=jnp.int32) * slot_len + starts
    row_index, in_span = compact_plan(row_base, lengths, CAP)
    safe_index = jnp.where(in_span, row_index, 0)
    compact_half = jnp.take(home_rows.reshape(per_dev * slot_len, half), safe_index, axis=0)

    rows_mine = lax.all_gather(compact_half, "req", axis=0, tiled=True)
    pairs = [(2 * k + j, 2 * k + 1 - j) for k in range(n_voc // 2) for j in range(2)]
    rows_other = lax.ppermute(rows_mine, "vocab", pairs)

    emb_mine = lax.dynamic_slice_in_dim(emb_piece, core * half, half, axis=1)
    emb_other = lax.dynamic_slice_in_dim(emb_piece, (1 - core) * half, half, axis=1)
    dims = (((1,), (1,)), ((), ()))
    logits = lax.dot_general(rows_mine, emb_mine, dims, preferred_element_type=jnp.float32)
    logits = logits + lax.dot_general(rows_other, emb_other, dims, preferred_element_type=jnp.float32)

    dealt_members = source_of.reshape(n_req, per_dev)
    dealt_lengths = jnp.take(all_lengths, dealt_members)
    dealt_offsets = jnp.cumsum(dealt_lengths, axis=1) - dealt_lengths
    dealt_starts = jnp.take(all_starts, dealt_members)
    member_targets = jnp.take(all_targets, source_of, axis=0).reshape(n_req, per_dev, slot_len)
    counter = jnp.arange(CAP, dtype=jnp.int32)
    source_pos = counter[None, None, :] - dealt_offsets[:, :, None] + dealt_starts[:, :, None]
    in_member = (counter[None, None, :] >= dealt_offsets[:, :, None]) & (
        counter[None, None, :] < (dealt_offsets + dealt_lengths)[:, :, None]
    )
    slot_ids = jnp.arange(slot_len, dtype=jnp.int32)
    hit = (source_pos[..., None] == slot_ids) & in_member[..., None]
    target_ids = jnp.sum(jnp.where(hit, member_targets[:, :, None, :], 0), axis=(1, 3)).reshape(-1)

    local_top = jnp.max(logits, axis=1)
    shifted = logits - local_top[:, None]
    weights = jnp.exp(shifted)
    local_mass = jnp.sum(weights, axis=1)
    local_spread = jnp.sum(weights * shifted, axis=1)
    local_ids = target_ids - (vhere * voc_local + here * piece)
    local_target = jnp.sum(
        jnp.where(jnp.arange(piece, dtype=jnp.int32)[None, :] == local_ids[:, None], logits, 0.0),
        axis=1,
    )

    def merge(stats):
        top_each, mass_each, spread_each, target_each = stats[:, 0], stats[:, 1], stats[:, 2], stats[:, 3]
        top = jnp.max(top_each, axis=0)
        gap = top_each - top[None]
        factor = jnp.exp(gap)
        mass = jnp.sum(factor * mass_each, axis=0)
        spread = jnp.sum(factor * (spread_each + gap * mass_each), axis=0)
        return jnp.stack([top, mass, spread, jnp.sum(target_each, axis=0)])

    offsets = dealt_offsets.reshape(-1)
    pos = jnp.arange(slot_len, dtype=jnp.int32)[None, :]
    local_stats = jnp.stack([local_top, local_mass, local_spread, local_target]).reshape(4, n_req, CAP)
    request_rows = jnp.take(local_stats, deal_order // per_dev, axis=1)
    at = (jnp.take(offsets, deal_order) - all_starts)[:, None] + pos
    pick = (jnp.arange(CAP, dtype=jnp.int32)[None, :, None] == at[:, None, :]).astype(jnp.float32)
    picked = lax.dot_general(
        request_rows.transpose(1, 0, 2),
        pick,
        (((2,), (1,)), ((0,), (0,))),
        precision=lax.Precision.HIGHEST,
        preferred_element_type=jnp.float32,
    )
    to_home = picked.reshape(n_req, per_dev, 4, slot_len).transpose(0, 2, 1, 3)
    by_req = merge(lax.all_to_all(to_home, "req", split_axis=0, concat_axis=0, tiled=True))
    row_top, row_mass, row_spread, row_target = merge(gather_by_all_to_all(by_req, "vocab", n_voc))
    log_mass = jnp.log(row_mass)

    my_reqs = here * per_dev + jnp.arange(per_dev, dtype=jnp.int32)
    my_start = jnp.take(all_starts, my_reqs)
    my_len = jnp.take(all_lengths, my_reqs)
    inside = (pos >= my_start[:, None]) & (pos < (my_start + my_len)[:, None])
    out_logprob = jnp.where(inside, row_target - row_top - log_mass, 0.0)
    out_entropy = jnp.where(inside, log_mass - row_spread / row_mass, 0.0)
    return (out_logprob, out_entropy)


def solution(mesh):
    in_specs = (
        P("req", None, None),
        P(),
        P("vocab", "req"),
        P("req", None),
        P("req"),
        P("req"),
        P(),
    )
    out_specs = (P("req", None), P("req", None))
    body = functools.partial(shards, mesh.shape["vocab"])
    return jax.shard_map(body, mesh=mesh, in_specs=in_specs, out_specs=out_specs, check_vma=False)
```

```python
import functools

import jax
import jax.numpy as jnp
from jax import lax
from jax.sharding import PartitionSpec as P

CAP = 224


eps = 1e-06


def compact_plan(row_base, lengths, capacity):
    offsets = jnp.cumsum(lengths) - lengths
    counter = jnp.arange(capacity, dtype=jnp.int32)
    member = jnp.sum((counter[:, None] >= offsets[None, :]).astype(jnp.int32), axis=1) - 1
    member_hot = (member[:, None] == jnp.arange(lengths.shape[0], dtype=jnp.int32)[None, :]).astype(
        jnp.int32
    )
    row_index = jnp.sum(member_hot * (row_base - offsets)[None, :], axis=1) + counter
    in_span = counter < jnp.sum(lengths)
    return (row_index, in_span)


def normalize(rows, gain):
    wide_rows = rows.astype(jnp.float32)
    scale = lax.rsqrt(jnp.mean(wide_rows * wide_rows, axis=-1, keepdims=True) + eps)
    return (wide_rows * scale * gain).astype(jnp.bfloat16)


def gather_by_all_to_all(x, axis, n):
    tiles = jnp.broadcast_to(x[None], (n,) + x.shape)
    return lax.all_to_all(tiles, axis, split_axis=0, concat_axis=0, tiled=True)


def shards(n_voc, hidden, gain, embedding, targets, span_start, span_len, deal_order):
    per_dev = hidden.shape[0]
    slot_len = hidden.shape[1]
    width = hidden.shape[2]
    total = deal_order.shape[0]
    n_req = total // per_dev
    voc_local = embedding.shape[0]
    piece = voc_local // n_req
    half = width // 2
    here = lax.axis_index("req")
    vhere = lax.axis_index("vocab")
    core = vhere % 2
    positions = jnp.arange(total, dtype=jnp.int32)
    source_of = jnp.sum(
        jnp.where(deal_order[None, :] == positions[:, None], positions[None, :], 0), axis=1
    )

    emb_chunks = embedding.reshape(n_req, piece, embedding.shape[1])
    emb_blocks = jnp.zeros_like(emb_chunks)
    emb_blocks = lax.dynamic_update_index_in_dim(
        emb_blocks, lax.dynamic_index_in_dim(emb_chunks, here, keepdims=False), here, 0
    )
    for shift in range(1, n_req):
        outgoing = lax.dynamic_index_in_dim(emb_chunks, (here + shift) % n_req, keepdims=False)
        perm = [(i, (i + shift) % n_req) for i in range(n_req)]
        incoming = lax.ppermute(outgoing, "req", perm)
        emb_blocks = lax.dynamic_update_index_in_dim(emb_blocks, incoming, (here - shift) % n_req, 0)
    emb_piece = emb_blocks.transpose(1, 0, 2).reshape(piece, width)

    normed_home = normalize(hidden, gain)
    my_half = lax.dynamic_slice_in_dim(normed_home, core * half, half, axis=2)
    block = slot_len // n_req
    digits = jnp.stack([targets // 16384, (targets // 128) % 128, targets % 128], axis=1)
    bounds = jnp.zeros((per_dev, 1, slot_len), jnp.int32)
    bounds = bounds.at[:, 0, 0].set(span_start).at[:, 0, 1].set(span_len)
    meta = jnp.concatenate([digits, bounds], axis=1).astype(jnp.bfloat16).reshape(per_dev, 1, 1, -1)
    meta = jnp.pad(meta, ((0, 0), (0, 0), (0, 0), (0, half - meta.shape[3])))
    blocks = jnp.concatenate(
        [my_half.reshape(per_dev, n_req, block, half), jnp.broadcast_to(meta, (per_dev, n_req, 1, half))],
        axis=2,
    ).transpose(1, 0, 2, 3)
    received = lax.all_to_all(blocks, "req", split_axis=0, concat_axis=0, tiled=True)
    spread_rows = received[:, :, :block].reshape(total, block, half)
    meta_all = received[:, :, block, : 4 * slot_len].astype(jnp.int32).reshape(total, 4, slot_len)
    all_targets = meta_all[:, 0] * 16384 + meta_all[:, 1] * 128 + meta_all[:, 2]
    all_starts = meta_all[:, 3, 0]
    all_lengths = meta_all[:, 3, 1]
    dealt_rows = jnp.take(spread_rows, source_of, axis=0)
    emb_piece, dealt_rows = lax.optimization_barrier((emb_piece, dealt_rows))
    home_rows = lax.all_to_all(dealt_rows, "req", split_axis=0, concat_axis=1, tiled=True)

    my_slots = here * per_dev + jnp.arange(per_dev, dtype=jnp.int32)
    members = jnp.take(source_of, my_slots)
    lengths = jnp.take(all_lengths, members)
    starts = jnp.take(all_starts, members)
    row_base = jnp.arange(per_dev, dtype=jnp.int32) * slot_len + starts
    row_index, in_span = compact_plan(row_base, lengths, CAP)
    safe_index = jnp.where(in_span, row_index, 0)
    compact_half = jnp.take(home_rows.reshape(per_dev * slot_len, half), safe_index, axis=0)

    rows_mine = lax.all_gather(compact_half, "req", axis=0, tiled=True)
    pairs = [(2 * k + j, 2 * k + 1 - j) for k in range(n_voc // 2) for j in range(2)]
    rows_other = lax.ppermute(rows_mine, "vocab", pairs)

    emb_mine = lax.dynamic_slice_in_dim(emb_piece, core * half, half, axis=1)
    emb_other = lax.dynamic_slice_in_dim(emb_piece, (1 - core) * half, half, axis=1)
    dims = (((1,), (1,)), ((), ()))
    logits = lax.dot_general(rows_mine, emb_mine, dims, preferred_element_type=jnp.float32)
    logits = logits + lax.dot_general(rows_other, emb_other, dims, preferred_element_type=jnp.float32)

    dealt_members = source_of.reshape(n_req, per_dev)
    dealt_lengths = jnp.take(all_lengths, dealt_members)
    dealt_offsets = jnp.cumsum(dealt_lengths, axis=1) - dealt_lengths
    dealt_starts = jnp.take(all_starts, dealt_members)
    member_targets = jnp.take(all_targets, source_of, axis=0).reshape(n_req, per_dev, slot_len)
    counter = jnp.arange(CAP, dtype=jnp.int32)
    source_pos = counter[None, None, :] - dealt_offsets[:, :, None] + dealt_starts[:, :, None]
    in_member = (counter[None, None, :] >= dealt_offsets[:, :, None]) & (
        counter[None, None, :] < (dealt_offsets + dealt_lengths)[:, :, None]
    )
    slot_ids = jnp.arange(slot_len, dtype=jnp.int32)
    hit = (source_pos[..., None] == slot_ids) & in_member[..., None]
    target_ids = jnp.sum(jnp.where(hit, member_targets[:, :, None, :], 0), axis=(1, 3)).reshape(-1)

    local_top = jnp.max(logits, axis=1)
    shifted = logits - local_top[:, None]
    weights = jnp.exp(shifted)
    local_mass = jnp.sum(weights, axis=1)
    local_spread = jnp.sum(weights * shifted, axis=1)
    local_ids = target_ids - (vhere * voc_local + here * piece)
    local_target = jnp.sum(
        jnp.where(jnp.arange(piece, dtype=jnp.int32)[None, :] == local_ids[:, None], logits, 0.0),
        axis=1,
    )

    def merge(stats):
        top_each, mass_each, spread_each, target_each = stats[:, 0], stats[:, 1], stats[:, 2], stats[:, 3]
        top = jnp.max(top_each, axis=0)
        gap = top_each - top[None]
        factor = jnp.exp(gap)
        mass = jnp.sum(factor * mass_each, axis=0)
        spread = jnp.sum(factor * (spread_each + gap * mass_each), axis=0)
        return jnp.stack([top, mass, spread, jnp.sum(target_each, axis=0)])

    offsets = dealt_offsets.reshape(-1)
    pos = jnp.arange(slot_len, dtype=jnp.int32)[None, :]
    local_stats = jnp.stack([local_top, local_mass, local_spread, local_target]).reshape(4, n_req, CAP)
    request_rows = jnp.take(local_stats, deal_order // per_dev, axis=1)
    at = (jnp.take(offsets, deal_order) - all_starts)[:, None] + pos
    pick = (jnp.arange(CAP, dtype=jnp.int32)[None, :, None] == at[:, None, :]).astype(jnp.float32)
    picked = lax.dot_general(
        request_rows.transpose(1, 0, 2),
        pick,
        (((2,), (1,)), ((0,), (0,))),
        precision=lax.Precision.HIGHEST,
        preferred_element_type=jnp.float32,
    )
    to_home = picked.reshape(n_req, per_dev, 4, slot_len).transpose(0, 2, 1, 3)
    by_req = merge(lax.all_to_all(to_home, "req", split_axis=0, concat_axis=0, tiled=True))
    row_top, row_mass, row_spread, row_target = merge(gather_by_all_to_all(by_req, "vocab", n_voc))
    log_mass = jnp.log(row_mass)

    my_reqs = here * per_dev + jnp.arange(per_dev, dtype=jnp.int32)
    my_start = jnp.take(all_starts, my_reqs)
    my_len = jnp.take(all_lengths, my_reqs)
    inside = (pos >= my_start[:, None]) & (pos < (my_start + my_len)[:, None])
    out_logprob = jnp.where(inside, row_target - row_top - log_mass, 0.0)
    out_entropy = jnp.where(inside, log_mass - row_spread / row_mass, 0.0)
    return (out_logprob, out_entropy)


def solution(mesh):
    in_specs = (
        P("req", None, None),
        P(),
        P("vocab", "req"),
        P("req", None),
        P("req"),
        P("req"),
        P(),
    )
    out_specs = (P("req", None), P("req", None))
    body = functools.partial(shards, mesh.shape["vocab"])
    return jax.shard_map(body, mesh=mesh, in_specs=in_specs, out_specs=out_specs, check_vma=False)
```

```python
import functools

import jax
import jax.numpy as jnp
from jax import lax
from jax.sharding import PartitionSpec as P

CAP = 224


eps = 1e-06


def compact_plan(row_base, lengths, capacity):
    offsets = jnp.cumsum(lengths) - lengths
    counter = jnp.arange(capacity, dtype=jnp.int32)
    member = jnp.sum((counter[:, None] >= offsets[None, :]).astype(jnp.int32), axis=1) - 1
    member_hot = (member[:, None] == jnp.arange(lengths.shape[0], dtype=jnp.int32)[None, :]).astype(
        jnp.int32
    )
    row_index = jnp.sum(member_hot * (row_base - offsets)[None, :], axis=1) + counter
    in_span = counter < jnp.sum(lengths)
    return (row_index, in_span)


def normalize(rows, gain):
    wide_rows = rows.astype(jnp.float32)
    scale = lax.rsqrt(jnp.mean(wide_rows * wide_rows, axis=-1, keepdims=True) + eps)
    return (wide_rows * scale * gain).astype(jnp.bfloat16)


def gather_by_all_to_all(x, axis, n):
    tiles = jnp.broadcast_to(x[None], (n,) + x.shape)
    return lax.all_to_all(tiles, axis, split_axis=0, concat_axis=0, tiled=True)


def shards(n_voc, hidden, gain, embedding, targets, span_start, span_len, deal_order):
    per_dev = hidden.shape[0]
    slot_len = hidden.shape[1]
    width = hidden.shape[2]
    total = deal_order.shape[0]
    n_req = total // per_dev
    voc_local = embedding.shape[0]
    piece = voc_local // n_req
    half = width // 2
    here = lax.axis_index("req")
    vhere = lax.axis_index("vocab")
    core = vhere % 2
    positions = jnp.arange(total, dtype=jnp.int32)
    source_of = jnp.sum(
        jnp.where(deal_order[None, :] == positions[:, None], positions[None, :], 0), axis=1
    )

    emb_chunks = embedding.reshape(n_req, piece, embedding.shape[1])
    by_shift = [lax.dynamic_index_in_dim(emb_chunks, here, keepdims=False)]
    for shift in range(1, n_req):
        outgoing = lax.dynamic_index_in_dim(emb_chunks, (here + shift) % n_req, keepdims=False)
        perm = [(i, (i + shift) % n_req) for i in range(n_req)]
        by_shift.append(lax.ppermute(outgoing, "req", perm))
    reverse = jnp.stack([by_shift[0]] + [by_shift[k] for k in range(n_req - 1, 0, -1)])
    doubled = jnp.concatenate([reverse, reverse], axis=0)
    emb_blocks = lax.dynamic_slice_in_dim(doubled, (n_req - here) % n_req, n_req, axis=0)
    emb_piece = emb_blocks.transpose(1, 0, 2).reshape(piece, width)

    normed_home = normalize(hidden, gain)
    my_half = lax.dynamic_slice_in_dim(normed_home, core * half, half, axis=2)
    block = slot_len // n_req
    digits = jnp.stack([targets // 16384, (targets // 128) % 128, targets % 128], axis=1)
    bounds = jnp.zeros((per_dev, 1, slot_len), jnp.int32)
    bounds = bounds.at[:, 0, 0].set(span_start).at[:, 0, 1].set(span_len)
    meta = jnp.concatenate([digits, bounds], axis=1).astype(jnp.bfloat16).reshape(per_dev, 1, 1, -1)
    meta = jnp.pad(meta, ((0, 0), (0, 0), (0, 0), (0, half - meta.shape[3])))
    blocks = jnp.concatenate(
        [my_half.reshape(per_dev, n_req, block, half), jnp.broadcast_to(meta, (per_dev, n_req, 1, half))],
        axis=2,
    ).transpose(1, 0, 2, 3)
    received = lax.all_to_all(blocks, "req", split_axis=0, concat_axis=0, tiled=True)
    spread_rows = received[:, :, :block].reshape(total, block, half)
    meta_all = received[:, :, block, : 4 * slot_len].astype(jnp.int32).reshape(total, 4, slot_len)
    all_targets = meta_all[:, 0] * 16384 + meta_all[:, 1] * 128 + meta_all[:, 2]
    all_starts = meta_all[:, 3, 0]
    all_lengths = meta_all[:, 3, 1]
    dealt_rows = jnp.take(spread_rows, source_of, axis=0)
    emb_piece, dealt_rows = lax.optimization_barrier((emb_piece, dealt_rows))
    home_rows = lax.all_to_all(dealt_rows, "req", split_axis=0, concat_axis=1, tiled=True)

    my_slots = here * per_dev + jnp.arange(per_dev, dtype=jnp.int32)
    members = jnp.take(source_of, my_slots)
    lengths = jnp.take(all_lengths, members)
    starts = jnp.take(all_starts, members)
    row_base = jnp.arange(per_dev, dtype=jnp.int32) * slot_len + starts
    row_index, in_span = compact_plan(row_base, lengths, CAP)
    safe_index = jnp.where(in_span, row_index, 0)
    compact_half = jnp.take(home_rows.reshape(per_dev * slot_len, half), safe_index, axis=0)

    rows_mine = lax.all_gather(compact_half, "req", axis=0, tiled=True)
    pairs = [(2 * k + j, 2 * k + 1 - j) for k in range(n_voc // 2) for j in range(2)]
    rows_other = lax.ppermute(rows_mine, "vocab", pairs)

    emb_mine = lax.dynamic_slice_in_dim(emb_piece, core * half, half, axis=1)
    emb_other = lax.dynamic_slice_in_dim(emb_piece, (1 - core) * half, half, axis=1)
    dims = (((1,), (1,)), ((), ()))
    logits = lax.dot_general(rows_mine, emb_mine, dims, preferred_element_type=jnp.float32)
    logits = logits + lax.dot_general(rows_other, emb_other, dims, preferred_element_type=jnp.float32)

    dealt_members = source_of.reshape(n_req, per_dev)
    dealt_lengths = jnp.take(all_lengths, dealt_members)
    dealt_offsets = jnp.cumsum(dealt_lengths, axis=1) - dealt_lengths
    dealt_starts = jnp.take(all_starts, dealt_members)
    member_targets = jnp.take(all_targets, source_of, axis=0).reshape(n_req, per_dev, slot_len)
    counter = jnp.arange(CAP, dtype=jnp.int32)
    source_pos = counter[None, None, :] - dealt_offsets[:, :, None] + dealt_starts[:, :, None]
    in_member = (counter[None, None, :] >= dealt_offsets[:, :, None]) & (
        counter[None, None, :] < (dealt_offsets + dealt_lengths)[:, :, None]
    )
    slot_ids = jnp.arange(slot_len, dtype=jnp.int32)
    hit = (source_pos[..., None] == slot_ids) & in_member[..., None]
    target_ids = jnp.sum(jnp.where(hit, member_targets[:, :, None, :], 0), axis=(1, 3)).reshape(-1)

    local_top = jnp.max(logits, axis=1)
    shifted = logits - local_top[:, None]
    weights = jnp.exp(shifted)
    local_mass = jnp.sum(weights, axis=1)
    local_spread = jnp.sum(weights * shifted, axis=1)
    local_ids = target_ids - (vhere * voc_local + here * piece)
    local_target = jnp.sum(
        jnp.where(jnp.arange(piece, dtype=jnp.int32)[None, :] == local_ids[:, None], logits, 0.0),
        axis=1,
    )

    def merge(stats):
        top_each, mass_each, spread_each, target_each = stats[:, 0], stats[:, 1], stats[:, 2], stats[:, 3]
        top = jnp.max(top_each, axis=0)
        gap = top_each - top[None]
        factor = jnp.exp(gap)
        mass = jnp.sum(factor * mass_each, axis=0)
        spread = jnp.sum(factor * (spread_each + gap * mass_each), axis=0)
        return jnp.stack([top, mass, spread, jnp.sum(target_each, axis=0)])

    offsets = dealt_offsets.reshape(-1)
    pos = jnp.arange(slot_len, dtype=jnp.int32)[None, :]
    local_stats = jnp.stack([local_top, local_mass, local_spread, local_target]).reshape(4, n_req, CAP)
    request_rows = jnp.take(local_stats, deal_order // per_dev, axis=1)
    at = (jnp.take(offsets, deal_order) - all_starts)[:, None] + pos
    pick = (jnp.arange(CAP, dtype=jnp.int32)[None, :, None] == at[:, None, :]).astype(jnp.float32)
    picked = lax.dot_general(
        request_rows.transpose(1, 0, 2),
        pick,
        (((2,), (1,)), ((0,), (0,))),
        precision=lax.Precision.HIGHEST,
        preferred_element_type=jnp.float32,
    )
    to_home = picked.reshape(n_req, per_dev, 4, slot_len).transpose(0, 2, 1, 3)
    by_req = merge(lax.all_to_all(to_home, "req", split_axis=0, concat_axis=0, tiled=True))
    row_top, row_mass, row_spread, row_target = merge(gather_by_all_to_all(by_req, "vocab", n_voc))
    log_mass = jnp.log(row_mass)

    my_reqs = here * per_dev + jnp.arange(per_dev, dtype=jnp.int32)
    my_start = jnp.take(all_starts, my_reqs)
    my_len = jnp.take(all_lengths, my_reqs)
    inside = (pos >= my_start[:, None]) & (pos < (my_start + my_len)[:, None])
    out_logprob = jnp.where(inside, row_target - row_top - log_mass, 0.0)
    out_entropy = jnp.where(inside, log_mass - row_spread / row_mass, 0.0)
    return (out_logprob, out_entropy)


def solution(mesh):
    in_specs = (
        P("req", None, None),
        P(),
        P("vocab", "req"),
        P("req", None),
        P("req"),
        P("req"),
        P(),
    )
    out_specs = (P("req", None), P("req", None))
    body = functools.partial(shards, mesh.shape["vocab"])
    return jax.shard_map(body, mesh=mesh, in_specs=in_specs, out_specs=out_specs, check_vma=False)
```

```python
import functools

import jax
import jax.numpy as jnp
from jax import lax
from jax.sharding import PartitionSpec as P
from jax.experimental import pallas as pl

CAP = 224


eps = 1e-06


def compact_plan(row_base, lengths, capacity):
    offsets = jnp.cumsum(lengths) - lengths
    counter = jnp.arange(capacity, dtype=jnp.int32)
    member = jnp.sum((counter[:, None] >= offsets[None, :]).astype(jnp.int32), axis=1) - 1
    member_hot = (member[:, None] == jnp.arange(lengths.shape[0], dtype=jnp.int32)[None, :]).astype(
        jnp.int32
    )
    row_index = jnp.sum(member_hot * (row_base - offsets)[None, :], axis=1) + counter
    in_span = counter < jnp.sum(lengths)
    return (row_index, in_span)


def normalize(rows, gain):
    wide_rows = rows.astype(jnp.float32)
    scale = lax.rsqrt(jnp.mean(wide_rows * wide_rows, axis=-1, keepdims=True) + eps)
    return (wide_rows * scale * gain).astype(jnp.bfloat16)


def gather_by_all_to_all(x, axis, n):
    tiles = jnp.broadcast_to(x[None], (n,) + x.shape)
    return lax.all_to_all(tiles, axis, split_axis=0, concat_axis=0, tiled=True)


def stats_kernel(ids_ref, mine_ref, other_ref, emb_mine_ref, emb_other_ref, out_ref):
    dims = (((1,), (1,)), ((), ()))
    logits = lax.dot_general(emb_mine_ref[...], mine_ref[...], dims, preferred_element_type=jnp.float32)
    logits = logits + lax.dot_general(
        emb_other_ref[...], other_ref[...], dims, preferred_element_type=jnp.float32
    )
    top = jnp.max(logits, axis=0, keepdims=True)
    shifted = logits - top
    weights = jnp.exp(shifted)
    vocab_ids = lax.broadcasted_iota(jnp.int32, logits.shape, 0)
    target = jnp.sum(jnp.where(vocab_ids == ids_ref[...], logits, 0.0), axis=0, keepdims=True)
    out_ref[0:1, :] = top
    out_ref[1:2, :] = jnp.sum(weights, axis=0, keepdims=True)
    out_ref[2:3, :] = jnp.sum(weights * shifted, axis=0, keepdims=True)
    out_ref[3:4, :] = target
    out_ref[4:8, :] = jnp.zeros((4, top.shape[1]), jnp.float32)


def row_stats(ids, rows_mine, rows_other, emb_mine, emb_other, tile=256):
    n_rows, feat = rows_mine.shape
    vocab = emb_mine.shape[0]
    return pl.pallas_call(
        stats_kernel,
        grid=(n_rows // tile,),
        in_specs=[
            pl.BlockSpec((1, tile), lambda i: (0, i)),
            pl.BlockSpec((tile, feat), lambda i: (i, 0)),
            pl.BlockSpec((tile, feat), lambda i: (i, 0)),
            pl.BlockSpec((vocab, feat), lambda i: (0, 0)),
            pl.BlockSpec((vocab, feat), lambda i: (0, 0)),
        ],
        out_specs=pl.BlockSpec((8, tile), lambda i: (0, i)),
        out_shape=jax.ShapeDtypeStruct((8, n_rows), jnp.float32),
    )(ids, rows_mine, rows_other, emb_mine, emb_other)


def shards(n_voc, hidden, gain, embedding, targets, span_start, span_len, deal_order):
    per_dev = hidden.shape[0]
    slot_len = hidden.shape[1]
    width = hidden.shape[2]
    total = deal_order.shape[0]
    n_req = total // per_dev
    voc_local = embedding.shape[0]
    piece = voc_local // n_req
    half = width // 2
    here = lax.axis_index("req")
    vhere = lax.axis_index("vocab")
    core = vhere % 2
    positions = jnp.arange(total, dtype=jnp.int32)
    source_of = jnp.sum(
        jnp.where(deal_order[None, :] == positions[:, None], positions[None, :], 0), axis=1
    )

    emb_piece = lax.all_to_all(embedding, "req", split_axis=0, concat_axis=1, tiled=True)

    normed_home = normalize(hidden, gain)
    my_half = lax.dynamic_slice_in_dim(normed_home, core * half, half, axis=2)
    block = slot_len // n_req
    digits = jnp.stack([targets // 16384, (targets // 128) % 128, targets % 128], axis=1)
    bounds = jnp.zeros((per_dev, 1, slot_len), jnp.int32)
    bounds = bounds.at[:, 0, 0].set(span_start).at[:, 0, 1].set(span_len)
    meta = jnp.concatenate([digits, bounds], axis=1).astype(jnp.bfloat16).reshape(per_dev, 1, 1, -1)
    meta = jnp.pad(meta, ((0, 0), (0, 0), (0, 0), (0, half - meta.shape[3])))
    blocks = jnp.concatenate(
        [my_half.reshape(per_dev, n_req, block, half), jnp.broadcast_to(meta, (per_dev, n_req, 1, half))],
        axis=2,
    ).transpose(1, 0, 2, 3)
    received = lax.all_to_all(blocks, "req", split_axis=0, concat_axis=0, tiled=True)
    spread_rows = received[:, :, :block].reshape(total, block, half)
    meta_all = received[:, :, block, : 4 * slot_len].astype(jnp.int32).reshape(total, 4, slot_len)
    all_targets = meta_all[:, 0] * 16384 + meta_all[:, 1] * 128 + meta_all[:, 2]
    all_starts = meta_all[:, 3, 0]
    all_lengths = meta_all[:, 3, 1]
    dealt_rows = jnp.take(spread_rows, source_of, axis=0)
    home_rows = lax.all_to_all(dealt_rows, "req", split_axis=0, concat_axis=1, tiled=True)

    my_slots = here * per_dev + jnp.arange(per_dev, dtype=jnp.int32)
    members = jnp.take(source_of, my_slots)
    lengths = jnp.take(all_lengths, members)
    starts = jnp.take(all_starts, members)
    row_base = jnp.arange(per_dev, dtype=jnp.int32) * slot_len + starts
    row_index, in_span = compact_plan(row_base, lengths, CAP)
    safe_index = jnp.where(in_span, row_index, 0)
    compact_half = jnp.take(home_rows.reshape(per_dev * slot_len, half), safe_index, axis=0)

    rows_mine = lax.all_gather(compact_half, "req", axis=0, tiled=True)
    pairs = [(2 * k + j, 2 * k + 1 - j) for k in range(n_voc // 2) for j in range(2)]
    rows_other = lax.ppermute(rows_mine, "vocab", pairs)

    emb_mine = lax.dynamic_slice_in_dim(emb_piece, core * half, half, axis=1)
    emb_other = lax.dynamic_slice_in_dim(emb_piece, (1 - core) * half, half, axis=1)
    dealt_members = source_of.reshape(n_req, per_dev)
    dealt_lengths = jnp.take(all_lengths, dealt_members)
    dealt_offsets = jnp.cumsum(dealt_lengths, axis=1) - dealt_lengths
    dealt_starts = jnp.take(all_starts, dealt_members)
    member_targets = jnp.take(all_targets, source_of, axis=0).reshape(n_req, per_dev, slot_len)
    counter = jnp.arange(CAP, dtype=jnp.int32)
    source_pos = counter[None, None, :] - dealt_offsets[:, :, None] + dealt_starts[:, :, None]
    in_member = (counter[None, None, :] >= dealt_offsets[:, :, None]) & (
        counter[None, None, :] < (dealt_offsets + dealt_lengths)[:, :, None]
    )
    slot_ids = jnp.arange(slot_len, dtype=jnp.int32)
    hit = (source_pos[..., None] == slot_ids) & in_member[..., None]
    target_ids = jnp.sum(jnp.where(hit, member_targets[:, :, None, :], 0), axis=(1, 3)).reshape(-1)

    local_ids = (target_ids - (vhere * voc_local + here * piece)).reshape(1, -1)
    local_stats = row_stats(local_ids, rows_mine, rows_other, emb_mine, emb_other)[:4]

    def merge(stats):
        top_each, mass_each, spread_each, target_each = stats[:, 0], stats[:, 1], stats[:, 2], stats[:, 3]
        top = jnp.max(top_each, axis=0)
        gap = top_each - top[None]
        factor = jnp.exp(gap)
        mass = jnp.sum(factor * mass_each, axis=0)
        spread = jnp.sum(factor * (spread_each + gap * mass_each), axis=0)
        return jnp.stack([top, mass, spread, jnp.sum(target_each, axis=0)])

    offsets = dealt_offsets.reshape(-1)
    pos = jnp.arange(slot_len, dtype=jnp.int32)[None, :]
    local_stats = local_stats.reshape(4, n_req, CAP)
    request_rows = jnp.take(local_stats, deal_order // per_dev, axis=1)
    at = (jnp.take(offsets, deal_order) - all_starts)[:, None] + pos
    pick = (jnp.arange(CAP, dtype=jnp.int32)[None, :, None] == at[:, None, :]).astype(jnp.float32)
    picked = lax.dot_general(
        request_rows.transpose(1, 0, 2),
        pick,
        (((2,), (1,)), ((0,), (0,))),
        precision=lax.Precision.HIGHEST,
        preferred_element_type=jnp.float32,
    )
    to_home = picked.reshape(n_req, per_dev, 4, slot_len).transpose(0, 2, 1, 3)
    by_req = merge(lax.all_to_all(to_home, "req", split_axis=0, concat_axis=0, tiled=True))
    row_top, row_mass, row_spread, row_target = merge(gather_by_all_to_all(by_req, "vocab", n_voc))
    log_mass = jnp.log(row_mass)

    my_reqs = here * per_dev + jnp.arange(per_dev, dtype=jnp.int32)
    my_start = jnp.take(all_starts, my_reqs)
    my_len = jnp.take(all_lengths, my_reqs)
    inside = (pos >= my_start[:, None]) & (pos < (my_start + my_len)[:, None])
    out_logprob = jnp.where(inside, row_target - row_top - log_mass, 0.0)
    out_entropy = jnp.where(inside, log_mass - row_spread / row_mass, 0.0)
    return (out_logprob, out_entropy)


def solution(mesh):
    in_specs = (
        P("req", None, None),
        P(),
        P("vocab", "req"),
        P("req", None),
        P("req"),
        P("req"),
        P(),
    )
    out_specs = (P("req", None), P("req", None))
    body = functools.partial(shards, mesh.shape["vocab"])
    return jax.shard_map(body, mesh=mesh, in_specs=in_specs, out_specs=out_specs, check_vma=False)
```

```python
import functools

import jax
import jax.numpy as jnp
from jax import lax
from jax.sharding import PartitionSpec as P
from jax.experimental import pallas as pl

CAP = 224


eps = 1e-06


def compact_plan(row_base, lengths, capacity):
    offsets = jnp.cumsum(lengths) - lengths
    counter = jnp.arange(capacity, dtype=jnp.int32)
    member = jnp.sum((counter[:, None] >= offsets[None, :]).astype(jnp.int32), axis=1) - 1
    member_hot = (member[:, None] == jnp.arange(lengths.shape[0], dtype=jnp.int32)[None, :]).astype(
        jnp.int32
    )
    row_index = jnp.sum(member_hot * (row_base - offsets)[None, :], axis=1) + counter
    in_span = counter < jnp.sum(lengths)
    return (row_index, in_span)


def normalize(rows, gain):
    wide_rows = rows.astype(jnp.float32)
    scale = lax.rsqrt(jnp.mean(wide_rows * wide_rows, axis=-1, keepdims=True) + eps)
    return (wide_rows * scale * gain).astype(jnp.bfloat16)


def gather_by_all_to_all(x, axis, n):
    tiles = jnp.broadcast_to(x[None], (n,) + x.shape)
    return lax.all_to_all(tiles, axis, split_axis=0, concat_axis=0, tiled=True)


def stats_kernel(ids_ref, mine_ref, other_ref, emb_mine_ref, emb_other_ref, out_ref):
    logits = jnp.dot(mine_ref[...], emb_mine_ref[...], preferred_element_type=jnp.float32)
    logits = logits + jnp.dot(other_ref[...], emb_other_ref[...], preferred_element_type=jnp.float32)
    top = jnp.max(logits, axis=1, keepdims=True)
    shifted = logits - top
    weights = jnp.exp(shifted)
    vocab_ids = lax.broadcasted_iota(jnp.int32, logits.shape, 1)
    target = jnp.sum(jnp.where(vocab_ids == ids_ref[...], logits, 0.0), axis=1, keepdims=True)
    out_ref[...] = jnp.concatenate(
        [
            top,
            jnp.sum(weights, axis=1, keepdims=True),
            jnp.sum(weights * shifted, axis=1, keepdims=True),
            target,
            jnp.zeros((top.shape[0], 4), jnp.float32),
        ],
        axis=1,
    )


def row_stats(ids, rows_mine, rows_other, emb_mine, emb_other, tile=512):
    n_rows, feat = rows_mine.shape
    vocab = emb_mine.shape[1]
    return pl.pallas_call(
        stats_kernel,
        grid=(n_rows // tile,),
        in_specs=[
            pl.BlockSpec((tile, 1), lambda i: (i, 0)),
            pl.BlockSpec((tile, feat), lambda i: (i, 0)),
            pl.BlockSpec((tile, feat), lambda i: (i, 0)),
            pl.BlockSpec((feat, vocab), lambda i: (0, 0)),
            pl.BlockSpec((feat, vocab), lambda i: (0, 0)),
        ],
        out_specs=pl.BlockSpec((tile, 8), lambda i: (i, 0)),
        out_shape=jax.ShapeDtypeStruct((n_rows, 8), jnp.float32),
    )(ids, rows_mine, rows_other, emb_mine, emb_other)


def shards(n_voc, hidden, gain, embedding, targets, span_start, span_len, deal_order):
    per_dev = hidden.shape[0]
    slot_len = hidden.shape[1]
    width = hidden.shape[2]
    total = deal_order.shape[0]
    n_req = total // per_dev
    voc_local = embedding.shape[0]
    piece = voc_local // n_req
    half = width // 2
    here = lax.axis_index("req")
    vhere = lax.axis_index("vocab")
    core = vhere % 2
    positions = jnp.arange(total, dtype=jnp.int32)
    source_of = jnp.sum(
        jnp.where(deal_order[None, :] == positions[:, None], positions[None, :], 0), axis=1
    )

    emb_piece = lax.all_to_all(embedding, "req", split_axis=0, concat_axis=1, tiled=True)

    normed_home = normalize(hidden, gain)
    my_half = lax.dynamic_slice_in_dim(normed_home, core * half, half, axis=2)
    block = slot_len // n_req
    digits = jnp.stack([targets // 16384, (targets // 128) % 128, targets % 128], axis=1)
    bounds = jnp.zeros((per_dev, 1, slot_len), jnp.int32)
    bounds = bounds.at[:, 0, 0].set(span_start).at[:, 0, 1].set(span_len)
    meta = jnp.concatenate([digits, bounds], axis=1).astype(jnp.bfloat16).reshape(per_dev, 1, 1, -1)
    meta = jnp.pad(meta, ((0, 0), (0, 0), (0, 0), (0, half - meta.shape[3])))
    blocks = jnp.concatenate(
        [my_half.reshape(per_dev, n_req, block, half), jnp.broadcast_to(meta, (per_dev, n_req, 1, half))],
        axis=2,
    ).transpose(1, 0, 2, 3)
    received = lax.all_to_all(blocks, "req", split_axis=0, concat_axis=0, tiled=True)
    spread_rows = received[:, :, :block].reshape(total, block, half)
    meta_all = received[:, :, block, : 4 * slot_len].astype(jnp.int32).reshape(total, 4, slot_len)
    all_targets = meta_all[:, 0] * 16384 + meta_all[:, 1] * 128 + meta_all[:, 2]
    all_starts = meta_all[:, 3, 0]
    all_lengths = meta_all[:, 3, 1]
    dealt_rows = jnp.take(spread_rows, source_of, axis=0)
    home_rows = lax.all_to_all(dealt_rows, "req", split_axis=0, concat_axis=1, tiled=True)

    my_slots = here * per_dev + jnp.arange(per_dev, dtype=jnp.int32)
    members = jnp.take(source_of, my_slots)
    lengths = jnp.take(all_lengths, members)
    starts = jnp.take(all_starts, members)
    row_base = jnp.arange(per_dev, dtype=jnp.int32) * slot_len + starts
    row_index, in_span = compact_plan(row_base, lengths, CAP)
    safe_index = jnp.where(in_span, row_index, 0)
    compact_half = jnp.take(home_rows.reshape(per_dev * slot_len, half), safe_index, axis=0)

    rows_mine = lax.all_gather(compact_half, "req", axis=0, tiled=True)
    pairs = [(2 * k + j, 2 * k + 1 - j) for k in range(n_voc // 2) for j in range(2)]
    rows_other = lax.ppermute(rows_mine, "vocab", pairs)

    emb_mine = lax.dynamic_slice_in_dim(emb_piece, core * half, half, axis=1)
    emb_other = lax.dynamic_slice_in_dim(emb_piece, (1 - core) * half, half, axis=1)
    dealt_members = source_of.reshape(n_req, per_dev)
    dealt_lengths = jnp.take(all_lengths, dealt_members)
    dealt_offsets = jnp.cumsum(dealt_lengths, axis=1) - dealt_lengths
    dealt_starts = jnp.take(all_starts, dealt_members)
    member_targets = jnp.take(all_targets, source_of, axis=0).reshape(n_req, per_dev, slot_len)
    counter = jnp.arange(CAP, dtype=jnp.int32)
    source_pos = counter[None, None, :] - dealt_offsets[:, :, None] + dealt_starts[:, :, None]
    in_member = (counter[None, None, :] >= dealt_offsets[:, :, None]) & (
        counter[None, None, :] < (dealt_offsets + dealt_lengths)[:, :, None]
    )
    slot_ids = jnp.arange(slot_len, dtype=jnp.int32)
    hit = (source_pos[..., None] == slot_ids) & in_member[..., None]
    target_ids = jnp.sum(jnp.where(hit, member_targets[:, :, None, :], 0), axis=(1, 3)).reshape(-1)

    local_ids = (target_ids - (vhere * voc_local + here * piece)).reshape(-1, 1)
    local_stats = row_stats(local_ids, rows_mine, rows_other, emb_mine.T, emb_other.T)[:, :4].T

    def merge(stats):
        top_each, mass_each, spread_each, target_each = stats[:, 0], stats[:, 1], stats[:, 2], stats[:, 3]
        top = jnp.max(top_each, axis=0)
        gap = top_each - top[None]
        factor = jnp.exp(gap)
        mass = jnp.sum(factor * mass_each, axis=0)
        spread = jnp.sum(factor * (spread_each + gap * mass_each), axis=0)
        return jnp.stack([top, mass, spread, jnp.sum(target_each, axis=0)])

    offsets = dealt_offsets.reshape(-1)
    pos = jnp.arange(slot_len, dtype=jnp.int32)[None, :]
    local_stats = local_stats.reshape(4, n_req, CAP)
    request_rows = jnp.take(local_stats, deal_order // per_dev, axis=1)
    at = (jnp.take(offsets, deal_order) - all_starts)[:, None] + pos
    pick = (jnp.arange(CAP, dtype=jnp.int32)[None, :, None] == at[:, None, :]).astype(jnp.float32)
    picked = lax.dot_general(
        request_rows.transpose(1, 0, 2),
        pick,
        (((2,), (1,)), ((0,), (0,))),
        precision=lax.Precision.HIGHEST,
        preferred_element_type=jnp.float32,
    )
    to_home = picked.reshape(n_req, per_dev, 4, slot_len).transpose(0, 2, 1, 3)
    by_req = merge(lax.all_to_all(to_home, "req", split_axis=0, concat_axis=0, tiled=True))
    row_top, row_mass, row_spread, row_target = merge(gather_by_all_to_all(by_req, "vocab", n_voc))
    log_mass = jnp.log(row_mass)

    my_reqs = here * per_dev + jnp.arange(per_dev, dtype=jnp.int32)
    my_start = jnp.take(all_starts, my_reqs)
    my_len = jnp.take(all_lengths, my_reqs)
    inside = (pos >= my_start[:, None]) & (pos < (my_start + my_len)[:, None])
    out_logprob = jnp.where(inside, row_target - row_top - log_mass, 0.0)
    out_entropy = jnp.where(inside, log_mass - row_spread / row_mass, 0.0)
    return (out_logprob, out_entropy)


def solution(mesh):
    in_specs = (
        P("req", None, None),
        P(),
        P("vocab", "req"),
        P("req", None),
        P("req"),
        P("req"),
        P(),
    )
    out_specs = (P("req", None), P("req", None))
    body = functools.partial(shards, mesh.shape["vocab"])
    return jax.shard_map(body, mesh=mesh, in_specs=in_specs, out_specs=out_specs, check_vma=False)
```

```python
import functools

import jax
import jax.numpy as jnp
from jax import lax
from jax.sharding import PartitionSpec as P
from jax.experimental import pallas as pl

CAP = 224


eps = 1e-06


def compact_plan(row_base, lengths, capacity):
    offsets = jnp.cumsum(lengths) - lengths
    counter = jnp.arange(capacity, dtype=jnp.int32)
    member = jnp.sum((counter[:, None] >= offsets[None, :]).astype(jnp.int32), axis=1) - 1
    member_hot = (member[:, None] == jnp.arange(lengths.shape[0], dtype=jnp.int32)[None, :]).astype(
        jnp.int32
    )
    row_index = jnp.sum(member_hot * (row_base - offsets)[None, :], axis=1) + counter
    in_span = counter < jnp.sum(lengths)
    return (row_index, in_span)


def normalize(rows, gain):
    wide_rows = rows.astype(jnp.float32)
    scale = lax.rsqrt(jnp.mean(wide_rows * wide_rows, axis=-1, keepdims=True) + eps)
    return (wide_rows * scale * gain).astype(jnp.bfloat16)


def gather_by_all_to_all(x, axis, n):
    tiles = jnp.broadcast_to(x[None], (n,) + x.shape)
    return lax.all_to_all(tiles, axis, split_axis=0, concat_axis=0, tiled=True)


def stats_kernel(ids_ref, mine_ref, other_ref, emb_mine_ref, emb_other_ref, out_ref):
    dims = (((1,), (1,)), ((), ()))
    logits = lax.dot_general(emb_mine_ref[...], mine_ref[...], dims, preferred_element_type=jnp.float32)
    logits = logits + lax.dot_general(
        emb_other_ref[...], other_ref[...], dims, preferred_element_type=jnp.float32
    )
    top = jnp.max(logits, axis=0, keepdims=True)
    shifted = logits - top
    weights = jnp.exp(shifted)
    vocab_ids = lax.broadcasted_iota(jnp.int32, logits.shape, 0)
    target = jnp.sum(jnp.where(vocab_ids == ids_ref[...], logits, 0.0), axis=0, keepdims=True)
    out_ref[0:1, :] = top
    out_ref[1:2, :] = jnp.sum(weights, axis=0, keepdims=True)
    out_ref[2:3, :] = jnp.sum(weights * shifted, axis=0, keepdims=True)
    out_ref[3:4, :] = target
    out_ref[4:8, :] = jnp.zeros((4, top.shape[1]), jnp.float32)


def row_stats(ids, rows_mine, rows_other, emb_mine, emb_other, tile=512):
    n_rows, feat = rows_mine.shape
    vocab = emb_mine.shape[0]
    return pl.pallas_call(
        stats_kernel,
        grid=(n_rows // tile,),
        in_specs=[
            pl.BlockSpec((1, tile), lambda i: (0, i)),
            pl.BlockSpec((tile, feat), lambda i: (i, 0)),
            pl.BlockSpec((tile, feat), lambda i: (i, 0)),
            pl.BlockSpec((vocab, feat), lambda i: (0, 0)),
            pl.BlockSpec((vocab, feat), lambda i: (0, 0)),
        ],
        out_specs=pl.BlockSpec((8, tile), lambda i: (0, i)),
        out_shape=jax.ShapeDtypeStruct((8, n_rows), jnp.float32),
    )(ids, rows_mine, rows_other, emb_mine, emb_other)


def shards(n_voc, hidden, gain, embedding, targets, span_start, span_len, deal_order):
    per_dev = hidden.shape[0]
    slot_len = hidden.shape[1]
    width = hidden.shape[2]
    total = deal_order.shape[0]
    n_req = total // per_dev
    voc_local = embedding.shape[0]
    piece = voc_local // n_req
    half = width // 2
    here = lax.axis_index("req")
    vhere = lax.axis_index("vocab")
    core = vhere % 2
    positions = jnp.arange(total, dtype=jnp.int32)
    source_of = jnp.sum(
        jnp.where(deal_order[None, :] == positions[:, None], positions[None, :], 0), axis=1
    )

    emb_piece = lax.all_to_all(embedding, "req", split_axis=0, concat_axis=1, tiled=True)

    normed_home = normalize(hidden, gain)
    my_half = lax.dynamic_slice_in_dim(normed_home, core * half, half, axis=2)
    block = slot_len // n_req
    digits = jnp.stack([targets // 16384, (targets // 128) % 128, targets % 128], axis=1)
    bounds = jnp.zeros((per_dev, 1, slot_len), jnp.int32)
    bounds = bounds.at[:, 0, 0].set(span_start).at[:, 0, 1].set(span_len)
    meta = jnp.concatenate([digits, bounds], axis=1).astype(jnp.bfloat16).reshape(per_dev, 1, 1, -1)
    meta = jnp.pad(meta, ((0, 0), (0, 0), (0, 0), (0, half - meta.shape[3])))
    blocks = jnp.concatenate(
        [my_half.reshape(per_dev, n_req, block, half), jnp.broadcast_to(meta, (per_dev, n_req, 1, half))],
        axis=2,
    ).transpose(1, 0, 2, 3)
    received = lax.all_to_all(blocks, "req", split_axis=0, concat_axis=0, tiled=True)
    spread_rows = received[:, :, :block].reshape(total, block, half)
    meta_all = received[:, :, block, : 4 * slot_len].astype(jnp.int32).reshape(total, 4, slot_len)
    all_targets = meta_all[:, 0] * 16384 + meta_all[:, 1] * 128 + meta_all[:, 2]
    all_starts = meta_all[:, 3, 0]
    all_lengths = meta_all[:, 3, 1]
    dealt_rows = jnp.take(spread_rows, source_of, axis=0)
    home_rows = lax.all_to_all(dealt_rows, "req", split_axis=0, concat_axis=1, tiled=True)

    my_slots = here * per_dev + jnp.arange(per_dev, dtype=jnp.int32)
    members = jnp.take(source_of, my_slots)
    lengths = jnp.take(all_lengths, members)
    starts = jnp.take(all_starts, members)
    row_base = jnp.arange(per_dev, dtype=jnp.int32) * slot_len + starts
    row_index, in_span = compact_plan(row_base, lengths, CAP)
    safe_index = jnp.where(in_span, row_index, 0)
    compact_half = jnp.take(home_rows.reshape(per_dev * slot_len, half), safe_index, axis=0)

    rows_mine = lax.all_gather(compact_half, "req", axis=0, tiled=True)
    pairs = [(2 * k + j, 2 * k + 1 - j) for k in range(n_voc // 2) for j in range(2)]
    rows_other = lax.ppermute(rows_mine, "vocab", pairs)

    emb_mine = lax.dynamic_slice_in_dim(emb_piece, core * half, half, axis=1)
    emb_other = lax.dynamic_slice_in_dim(emb_piece, (1 - core) * half, half, axis=1)
    dealt_members = source_of.reshape(n_req, per_dev)
    dealt_lengths = jnp.take(all_lengths, dealt_members)
    dealt_offsets = jnp.cumsum(dealt_lengths, axis=1) - dealt_lengths
    dealt_starts = jnp.take(all_starts, dealt_members)
    member_targets = jnp.take(all_targets, source_of, axis=0).reshape(n_req, per_dev, slot_len)
    counter = jnp.arange(CAP, dtype=jnp.int32)
    source_pos = counter[None, None, :] - dealt_offsets[:, :, None] + dealt_starts[:, :, None]
    in_member = (counter[None, None, :] >= dealt_offsets[:, :, None]) & (
        counter[None, None, :] < (dealt_offsets + dealt_lengths)[:, :, None]
    )
    slot_ids = jnp.arange(slot_len, dtype=jnp.int32)
    hit = (source_pos[..., None] == slot_ids) & in_member[..., None]
    target_ids = jnp.sum(jnp.where(hit, member_targets[:, :, None, :], 0), axis=(1, 3)).reshape(-1)

    local_ids = (target_ids - (vhere * voc_local + here * piece)).reshape(1, -1)
    local_stats = row_stats(local_ids, rows_mine, rows_other, emb_mine, emb_other)[:4]

    def merge(stats):
        top_each, mass_each, spread_each, target_each = stats[:, 0], stats[:, 1], stats[:, 2], stats[:, 3]
        top = jnp.max(top_each, axis=0)
        gap = top_each - top[None]
        factor = jnp.exp(gap)
        mass = jnp.sum(factor * mass_each, axis=0)
        spread = jnp.sum(factor * (spread_each + gap * mass_each), axis=0)
        return jnp.stack([top, mass, spread, jnp.sum(target_each, axis=0)])

    offsets = dealt_offsets.reshape(-1)
    pos = jnp.arange(slot_len, dtype=jnp.int32)[None, :]
    local_stats = local_stats.reshape(4, n_req, CAP)
    request_rows = jnp.take(local_stats, deal_order // per_dev, axis=1)
    at = (jnp.take(offsets, deal_order) - all_starts)[:, None] + pos
    pick = (jnp.arange(CAP, dtype=jnp.int32)[None, :, None] == at[:, None, :]).astype(jnp.float32)
    picked = lax.dot_general(
        request_rows.transpose(1, 0, 2),
        pick,
        (((2,), (1,)), ((0,), (0,))),
        precision=lax.Precision.HIGHEST,
        preferred_element_type=jnp.float32,
    )
    to_home = picked.reshape(n_req, per_dev, 4, slot_len).transpose(0, 2, 1, 3)
    by_req = merge(lax.all_to_all(to_home, "req", split_axis=0, concat_axis=0, tiled=True))
    row_top, row_mass, row_spread, row_target = merge(gather_by_all_to_all(by_req, "vocab", n_voc))
    log_mass = jnp.log(row_mass)

    my_reqs = here * per_dev + jnp.arange(per_dev, dtype=jnp.int32)
    my_start = jnp.take(all_starts, my_reqs)
    my_len = jnp.take(all_lengths, my_reqs)
    inside = (pos >= my_start[:, None]) & (pos < (my_start + my_len)[:, None])
    out_logprob = jnp.where(inside, row_target - row_top - log_mass, 0.0)
    out_entropy = jnp.where(inside, log_mass - row_spread / row_mass, 0.0)
    return (out_logprob, out_entropy)


def solution(mesh):
    in_specs = (
        P("req", None, None),
        P(),
        P("vocab", "req"),
        P("req", None),
        P("req"),
        P("req"),
        P(),
    )
    out_specs = (P("req", None), P("req", None))
    body = functools.partial(shards, mesh.shape["vocab"])
    return jax.shard_map(body, mesh=mesh, in_specs=in_specs, out_specs=out_specs, check_vma=False)
```

```python
import functools

import jax
import jax.numpy as jnp
from jax import lax
from jax.sharding import PartitionSpec as P
from jax.experimental import pallas as pl

CAP = 224


eps = 1e-06


def compact_plan(row_base, lengths, capacity):
    offsets = jnp.cumsum(lengths) - lengths
    counter = jnp.arange(capacity, dtype=jnp.int32)
    member = jnp.sum((counter[:, None] >= offsets[None, :]).astype(jnp.int32), axis=1) - 1
    member_hot = (member[:, None] == jnp.arange(lengths.shape[0], dtype=jnp.int32)[None, :]).astype(
        jnp.int32
    )
    row_index = jnp.sum(member_hot * (row_base - offsets)[None, :], axis=1) + counter
    in_span = counter < jnp.sum(lengths)
    return (row_index, in_span)


def normalize(rows, gain):
    wide_rows = rows.astype(jnp.float32)
    scale = lax.rsqrt(jnp.mean(wide_rows * wide_rows, axis=-1, keepdims=True) + eps)
    return (wide_rows * scale * gain).astype(jnp.bfloat16)


def gather_by_all_to_all(x, axis, n):
    tiles = jnp.broadcast_to(x[None], (n,) + x.shape)
    return lax.all_to_all(tiles, axis, split_axis=0, concat_axis=0, tiled=True)


def stats_kernel(ids_ref, mine_ref, other_ref, emb_mine_ref, emb_other_ref, out_ref):
    dims = (((1,), (1,)), ((), ()))
    logits = lax.dot_general(emb_mine_ref[...], mine_ref[...], dims, preferred_element_type=jnp.float32)
    logits = logits + lax.dot_general(
        emb_other_ref[...], other_ref[...], dims, preferred_element_type=jnp.float32
    )
    top = jnp.max(logits, axis=0, keepdims=True)
    shifted = logits - top
    weights = jnp.exp(shifted)
    vocab_ids = lax.broadcasted_iota(jnp.int32, logits.shape, 0)
    target = jnp.sum(jnp.where(vocab_ids == ids_ref[...], logits, 0.0), axis=0, keepdims=True)
    out_ref[0:1, :] = top
    out_ref[1:2, :] = jnp.sum(weights, axis=0, keepdims=True)
    out_ref[2:3, :] = jnp.sum(weights * shifted, axis=0, keepdims=True)
    out_ref[3:4, :] = target
    out_ref[4:8, :] = jnp.zeros((4, top.shape[1]), jnp.float32)


def row_stats(ids, rows_mine, rows_other, emb_mine, emb_other, tile=896):
    n_rows, feat = rows_mine.shape
    vocab = emb_mine.shape[0]
    return pl.pallas_call(
        stats_kernel,
        grid=(n_rows // tile,),
        in_specs=[
            pl.BlockSpec((1, tile), lambda i: (0, i)),
            pl.BlockSpec((tile, feat), lambda i: (i, 0)),
            pl.BlockSpec((tile, feat), lambda i: (i, 0)),
            pl.BlockSpec((vocab, feat), lambda i: (0, 0)),
            pl.BlockSpec((vocab, feat), lambda i: (0, 0)),
        ],
        out_specs=pl.BlockSpec((8, tile), lambda i: (0, i)),
        out_shape=jax.ShapeDtypeStruct((8, n_rows), jnp.float32),
    )(ids, rows_mine, rows_other, emb_mine, emb_other)


def shards(n_voc, hidden, gain, embedding, targets, span_start, span_len, deal_order):
    per_dev = hidden.shape[0]
    slot_len = hidden.shape[1]
    width = hidden.shape[2]
    total = deal_order.shape[0]
    n_req = total // per_dev
    voc_local = embedding.shape[0]
    piece = voc_local // n_req
    half = width // 2
    here = lax.axis_index("req")
    vhere = lax.axis_index("vocab")
    core = vhere % 2
    positions = jnp.arange(total, dtype=jnp.int32)
    source_of = jnp.sum(
        jnp.where(deal_order[None, :] == positions[:, None], positions[None, :], 0), axis=1
    )

    emb_piece = lax.all_to_all(embedding, "req", split_axis=0, concat_axis=1, tiled=True)

    normed_home = normalize(hidden, gain)
    my_half = lax.dynamic_slice_in_dim(normed_home, core * half, half, axis=2)
    block = slot_len // n_req
    digits = jnp.stack([targets // 16384, (targets // 128) % 128, targets % 128], axis=1)
    bounds = jnp.zeros((per_dev, 1, slot_len), jnp.int32)
    bounds = bounds.at[:, 0, 0].set(span_start).at[:, 0, 1].set(span_len)
    meta = jnp.concatenate([digits, bounds], axis=1).astype(jnp.bfloat16).reshape(per_dev, 1, 1, -1)
    meta = jnp.pad(meta, ((0, 0), (0, 0), (0, 0), (0, half - meta.shape[3])))
    blocks = jnp.concatenate(
        [my_half.reshape(per_dev, n_req, block, half), jnp.broadcast_to(meta, (per_dev, n_req, 1, half))],
        axis=2,
    ).transpose(1, 0, 2, 3)
    received = lax.all_to_all(blocks, "req", split_axis=0, concat_axis=0, tiled=True)
    spread_rows = received[:, :, :block].reshape(total, block, half)
    meta_all = received[:, :, block, : 4 * slot_len].astype(jnp.int32).reshape(total, 4, slot_len)
    all_targets = meta_all[:, 0] * 16384 + meta_all[:, 1] * 128 + meta_all[:, 2]
    all_starts = meta_all[:, 3, 0]
    all_lengths = meta_all[:, 3, 1]
    dealt_rows = jnp.take(spread_rows, source_of, axis=0)
    home_rows = lax.all_to_all(dealt_rows, "req", split_axis=0, concat_axis=1, tiled=True)

    my_slots = here * per_dev + jnp.arange(per_dev, dtype=jnp.int32)
    members = jnp.take(source_of, my_slots)
    lengths = jnp.take(all_lengths, members)
    starts = jnp.take(all_starts, members)
    row_base = jnp.arange(per_dev, dtype=jnp.int32) * slot_len + starts
    row_index, in_span = compact_plan(row_base, lengths, CAP)
    safe_index = jnp.where(in_span, row_index, 0)
    compact_half = jnp.take(home_rows.reshape(per_dev * slot_len, half), safe_index, axis=0)

    rows_mine = lax.all_gather(compact_half, "req", axis=0, tiled=True)
    pairs = [(2 * k + j, 2 * k + 1 - j) for k in range(n_voc // 2) for j in range(2)]
    rows_other = lax.ppermute(rows_mine, "vocab", pairs)

    emb_mine = lax.dynamic_slice_in_dim(emb_piece, core * half, half, axis=1)
    emb_other = lax.dynamic_slice_in_dim(emb_piece, (1 - core) * half, half, axis=1)
    dealt_members = source_of.reshape(n_req, per_dev)
    dealt_lengths = jnp.take(all_lengths, dealt_members)
    dealt_offsets = jnp.cumsum(dealt_lengths, axis=1) - dealt_lengths
    dealt_starts = jnp.take(all_starts, dealt_members)
    member_targets = jnp.take(all_targets, source_of, axis=0).reshape(n_req, per_dev, slot_len)
    counter = jnp.arange(CAP, dtype=jnp.int32)
    source_pos = counter[None, None, :] - dealt_offsets[:, :, None] + dealt_starts[:, :, None]
    in_member = (counter[None, None, :] >= dealt_offsets[:, :, None]) & (
        counter[None, None, :] < (dealt_offsets + dealt_lengths)[:, :, None]
    )
    slot_ids = jnp.arange(slot_len, dtype=jnp.int32)
    hit = (source_pos[..., None] == slot_ids) & in_member[..., None]
    target_ids = jnp.sum(jnp.where(hit, member_targets[:, :, None, :], 0), axis=(1, 3)).reshape(-1)

    local_ids = (target_ids - (vhere * voc_local + here * piece)).reshape(1, -1)
    local_stats = row_stats(local_ids, rows_mine, rows_other, emb_mine, emb_other)[:4]

    def merge(stats):
        top_each, mass_each, spread_each, target_each = stats[:, 0], stats[:, 1], stats[:, 2], stats[:, 3]
        top = jnp.max(top_each, axis=0)
        gap = top_each - top[None]
        factor = jnp.exp(gap)
        mass = jnp.sum(factor * mass_each, axis=0)
        spread = jnp.sum(factor * (spread_each + gap * mass_each), axis=0)
        return jnp.stack([top, mass, spread, jnp.sum(target_each, axis=0)])

    offsets = dealt_offsets.reshape(-1)
    pos = jnp.arange(slot_len, dtype=jnp.int32)[None, :]
    local_stats = local_stats.reshape(4, n_req, CAP)
    request_rows = jnp.take(local_stats, deal_order // per_dev, axis=1)
    at = (jnp.take(offsets, deal_order) - all_starts)[:, None] + pos
    pick = (jnp.arange(CAP, dtype=jnp.int32)[None, :, None] == at[:, None, :]).astype(jnp.float32)
    picked = lax.dot_general(
        request_rows.transpose(1, 0, 2),
        pick,
        (((2,), (1,)), ((0,), (0,))),
        precision=lax.Precision.HIGHEST,
        preferred_element_type=jnp.float32,
    )
    to_home = picked.reshape(n_req, per_dev, 4, slot_len).transpose(0, 2, 1, 3)
    by_req = merge(lax.all_to_all(to_home, "req", split_axis=0, concat_axis=0, tiled=True))
    row_top, row_mass, row_spread, row_target = merge(gather_by_all_to_all(by_req, "vocab", n_voc))
    log_mass = jnp.log(row_mass)

    my_reqs = here * per_dev + jnp.arange(per_dev, dtype=jnp.int32)
    my_start = jnp.take(all_starts, my_reqs)
    my_len = jnp.take(all_lengths, my_reqs)
    inside = (pos >= my_start[:, None]) & (pos < (my_start + my_len)[:, None])
    out_logprob = jnp.where(inside, row_target - row_top - log_mass, 0.0)
    out_entropy = jnp.where(inside, log_mass - row_spread / row_mass, 0.0)
    return (out_logprob, out_entropy)


def solution(mesh):
    in_specs = (
        P("req", None, None),
        P(),
        P("vocab", "req"),
        P("req", None),
        P("req"),
        P("req"),
        P(),
    )
    out_specs = (P("req", None), P("req", None))
    body = functools.partial(shards, mesh.shape["vocab"])
    return jax.shard_map(body, mesh=mesh, in_specs=in_specs, out_specs=out_specs, check_vma=False)
```

```python
import functools

import jax
import jax.numpy as jnp
from jax import lax
from jax.sharding import PartitionSpec as P
from jax.experimental import pallas as pl

CAP = 224


eps = 1e-06


def compact_plan(row_base, lengths, capacity):
    offsets = jnp.cumsum(lengths) - lengths
    counter = jnp.arange(capacity, dtype=jnp.int32)
    member = jnp.sum((counter[:, None] >= offsets[None, :]).astype(jnp.int32), axis=1) - 1
    member_hot = (member[:, None] == jnp.arange(lengths.shape[0], dtype=jnp.int32)[None, :]).astype(
        jnp.int32
    )
    row_index = jnp.sum(member_hot * (row_base - offsets)[None, :], axis=1) + counter
    in_span = counter < jnp.sum(lengths)
    return (row_index, in_span)


def normalize(rows, gain):
    wide_rows = rows.astype(jnp.float32)
    scale = lax.rsqrt(jnp.mean(wide_rows * wide_rows, axis=-1, keepdims=True) + eps)
    return (wide_rows * scale * gain).astype(jnp.bfloat16)


def gather_by_all_to_all(x, axis, n):
    tiles = jnp.broadcast_to(x[None], (n,) + x.shape)
    return lax.all_to_all(tiles, axis, split_axis=0, concat_axis=0, tiled=True)


def stats_kernel(ids_ref, mine_ref, other_ref, emb_mine_ref, emb_other_ref, out_ref):
    dims = (((1,), (1,)), ((), ()))
    logits = lax.dot_general(emb_mine_ref[...], mine_ref[...], dims, preferred_element_type=jnp.float32)
    logits = logits + lax.dot_general(
        emb_other_ref[...], other_ref[...], dims, preferred_element_type=jnp.float32
    )
    top = jnp.max(logits, axis=0, keepdims=True)
    shifted = logits - top
    weights = jnp.exp(shifted)
    vocab_ids = lax.broadcasted_iota(jnp.int32, logits.shape, 0)
    target = jnp.sum(jnp.where(vocab_ids == ids_ref[...], logits, 0.0), axis=0, keepdims=True)
    out_ref[0:1, :] = top
    out_ref[1:2, :] = jnp.sum(weights, axis=0, keepdims=True)
    out_ref[2:3, :] = jnp.sum(weights * shifted, axis=0, keepdims=True)
    out_ref[3:4, :] = target
    out_ref[4:8, :] = jnp.zeros((4, top.shape[1]), jnp.float32)


def row_stats(ids, rows_mine, rows_other, emb_mine, emb_other, tile=512):
    n_rows, feat = rows_mine.shape
    vocab = emb_mine.shape[0]
    return pl.pallas_call(
        stats_kernel,
        grid=(n_rows // tile,),
        in_specs=[
            pl.BlockSpec((1, tile), lambda i: (0, i)),
            pl.BlockSpec((tile, feat), lambda i: (i, 0)),
            pl.BlockSpec((tile, feat), lambda i: (i, 0)),
            pl.BlockSpec((vocab, feat), lambda i: (0, 0)),
            pl.BlockSpec((vocab, feat), lambda i: (0, 0)),
        ],
        out_specs=pl.BlockSpec((8, tile), lambda i: (0, i)),
        out_shape=jax.ShapeDtypeStruct((8, n_rows), jnp.float32),
    )(ids, rows_mine, rows_other, emb_mine, emb_other)


def shards(n_voc, hidden, gain, embedding, targets, span_start, span_len, deal_order):
    per_dev = hidden.shape[0]
    slot_len = hidden.shape[1]
    width = hidden.shape[2]
    total = deal_order.shape[0]
    n_req = total // per_dev
    voc_local = embedding.shape[0]
    piece = voc_local // n_req
    half = width // 2
    here = lax.axis_index("req")
    vhere = lax.axis_index("vocab")
    core = vhere % 2
    positions = jnp.arange(total, dtype=jnp.int32)
    source_of = jnp.sum(
        jnp.where(deal_order[None, :] == positions[:, None], positions[None, :], 0), axis=1
    )

    emb_piece = lax.all_to_all(embedding, "req", split_axis=0, concat_axis=1, tiled=True)

    wide = hidden.astype(jnp.float32)
    scale = lax.rsqrt(jnp.mean(wide * wide, axis=-1, keepdims=True) + eps)
    half_rows = lax.dynamic_slice_in_dim(hidden, core * half, half, axis=2).astype(jnp.float32)
    half_gain = lax.dynamic_slice_in_dim(gain, core * half, half)
    my_half = (half_rows * scale * half_gain).astype(jnp.bfloat16)
    block = slot_len // n_req
    digits = jnp.stack([targets // 16384, (targets // 128) % 128, targets % 128], axis=1)
    bounds = jnp.zeros((per_dev, 1, slot_len), jnp.int32)
    bounds = bounds.at[:, 0, 0].set(span_start).at[:, 0, 1].set(span_len)
    meta = jnp.concatenate([digits, bounds], axis=1).astype(jnp.bfloat16).reshape(per_dev, 1, 1, -1)
    meta = jnp.pad(meta, ((0, 0), (0, 0), (0, 0), (0, half - meta.shape[3])))
    blocks = jnp.concatenate(
        [my_half.reshape(per_dev, n_req, block, half), jnp.broadcast_to(meta, (per_dev, n_req, 1, half))],
        axis=2,
    ).transpose(1, 0, 2, 3)
    received = lax.all_to_all(blocks, "req", split_axis=0, concat_axis=0, tiled=True)
    spread_rows = received[:, :, :block].reshape(total, block, half)
    meta_all = received[:, :, block, : 4 * slot_len].astype(jnp.int32).reshape(total, 4, slot_len)
    all_targets = meta_all[:, 0] * 16384 + meta_all[:, 1] * 128 + meta_all[:, 2]
    all_starts = meta_all[:, 3, 0]
    all_lengths = meta_all[:, 3, 1]
    dealt_rows = jnp.take(spread_rows, source_of, axis=0)
    home_rows = lax.all_to_all(dealt_rows, "req", split_axis=0, concat_axis=1, tiled=True)

    my_slots = here * per_dev + jnp.arange(per_dev, dtype=jnp.int32)
    members = jnp.take(source_of, my_slots)
    lengths = jnp.take(all_lengths, members)
    starts = jnp.take(all_starts, members)
    row_base = jnp.arange(per_dev, dtype=jnp.int32) * slot_len + starts
    row_index, in_span = compact_plan(row_base, lengths, CAP)
    safe_index = jnp.where(in_span, row_index, 0)
    compact_half = jnp.take(home_rows.reshape(per_dev * slot_len, half), safe_index, axis=0)

    rows_mine = lax.all_gather(compact_half, "req", axis=0, tiled=True)
    pairs = [(2 * k + j, 2 * k + 1 - j) for k in range(n_voc // 2) for j in range(2)]
    rows_other = lax.ppermute(rows_mine, "vocab", pairs)

    emb_mine = lax.dynamic_slice_in_dim(emb_piece, core * half, half, axis=1)
    emb_other = lax.dynamic_slice_in_dim(emb_piece, (1 - core) * half, half, axis=1)
    dealt_members = source_of.reshape(n_req, per_dev)
    dealt_lengths = jnp.take(all_lengths, dealt_members)
    dealt_offsets = jnp.cumsum(dealt_lengths, axis=1) - dealt_lengths
    dealt_starts = jnp.take(all_starts, dealt_members)
    member_targets = jnp.take(all_targets, source_of, axis=0).reshape(n_req, per_dev, slot_len)
    counter = jnp.arange(CAP, dtype=jnp.int32)
    source_pos = counter[None, None, :] - dealt_offsets[:, :, None] + dealt_starts[:, :, None]
    in_member = (counter[None, None, :] >= dealt_offsets[:, :, None]) & (
        counter[None, None, :] < (dealt_offsets + dealt_lengths)[:, :, None]
    )
    slot_ids = jnp.arange(slot_len, dtype=jnp.int32)
    hit = (source_pos[..., None] == slot_ids) & in_member[..., None]
    target_ids = jnp.sum(jnp.where(hit, member_targets[:, :, None, :], 0), axis=(1, 3)).reshape(-1)

    local_ids = (target_ids - (vhere * voc_local + here * piece)).reshape(1, -1)
    local_stats = row_stats(local_ids, rows_mine, rows_other, emb_mine, emb_other)[:4]

    def merge(stats):
        top_each, mass_each, spread_each, target_each = stats[:, 0], stats[:, 1], stats[:, 2], stats[:, 3]
        top = jnp.max(top_each, axis=0)
        gap = top_each - top[None]
        factor = jnp.exp(gap)
        mass = jnp.sum(factor * mass_each, axis=0)
        spread = jnp.sum(factor * (spread_each + gap * mass_each), axis=0)
        return jnp.stack([top, mass, spread, jnp.sum(target_each, axis=0)])

    offsets = dealt_offsets.reshape(-1)
    pos = jnp.arange(slot_len, dtype=jnp.int32)[None, :]
    local_stats = local_stats.reshape(4, n_req, CAP)
    request_rows = jnp.take(local_stats, deal_order // per_dev, axis=1)
    at = (jnp.take(offsets, deal_order) - all_starts)[:, None] + pos
    pick = (jnp.arange(CAP, dtype=jnp.int32)[None, :, None] == at[:, None, :]).astype(jnp.float32)
    picked = lax.dot_general(
        request_rows.transpose(1, 0, 2),
        pick,
        (((2,), (1,)), ((0,), (0,))),
        precision=lax.Precision.HIGHEST,
        preferred_element_type=jnp.float32,
    )
    to_home = picked.reshape(n_req, per_dev, 4, slot_len).transpose(0, 2, 1, 3)
    by_req = merge(lax.all_to_all(to_home, "req", split_axis=0, concat_axis=0, tiled=True))
    row_top, row_mass, row_spread, row_target = merge(gather_by_all_to_all(by_req, "vocab", n_voc))
    log_mass = jnp.log(row_mass)

    my_reqs = here * per_dev + jnp.arange(per_dev, dtype=jnp.int32)
    my_start = jnp.take(all_starts, my_reqs)
    my_len = jnp.take(all_lengths, my_reqs)
    inside = (pos >= my_start[:, None]) & (pos < (my_start + my_len)[:, None])
    out_logprob = jnp.where(inside, row_target - row_top - log_mass, 0.0)
    out_entropy = jnp.where(inside, log_mass - row_spread / row_mass, 0.0)
    return (out_logprob, out_entropy)


def solution(mesh):
    in_specs = (
        P("req", None, None),
        P(),
        P("vocab", "req"),
        P("req", None),
        P("req"),
        P("req"),
        P(),
    )
    out_specs = (P("req", None), P("req", None))
    body = functools.partial(shards, mesh.shape["vocab"])
    return jax.shard_map(body, mesh=mesh, in_specs=in_specs, out_specs=out_specs, check_vma=False)
```

```python
import functools

import jax
import jax.numpy as jnp
from jax import lax
from jax.sharding import PartitionSpec as P
from jax.experimental import pallas as pl

CAP = 224


eps = 1e-06


def compact_plan(row_base, lengths, capacity):
    offsets = jnp.cumsum(lengths) - lengths
    counter = jnp.arange(capacity, dtype=jnp.int32)
    member = jnp.sum((counter[:, None] >= offsets[None, :]).astype(jnp.int32), axis=1) - 1
    member_hot = (member[:, None] == jnp.arange(lengths.shape[0], dtype=jnp.int32)[None, :]).astype(
        jnp.int32
    )
    row_index = jnp.sum(member_hot * (row_base - offsets)[None, :], axis=1) + counter
    in_span = counter < jnp.sum(lengths)
    return (row_index, in_span)


def normalize(rows, gain):
    wide_rows = rows.astype(jnp.float32)
    scale = lax.rsqrt(jnp.mean(wide_rows * wide_rows, axis=-1, keepdims=True) + eps)
    return (wide_rows * scale * gain).astype(jnp.bfloat16)


def gather_by_all_to_all(x, axis, n):
    tiles = jnp.broadcast_to(x[None], (n,) + x.shape)
    return lax.all_to_all(tiles, axis, split_axis=0, concat_axis=0, tiled=True)


def stats_kernel(ids_ref, mine_ref, other_ref, emb_mine_ref, emb_other_ref, out_ref):
    dims = (((1,), (1,)), ((), ()))
    logits = lax.dot_general(emb_mine_ref[...], mine_ref[...], dims, preferred_element_type=jnp.float32)
    logits = logits + lax.dot_general(
        emb_other_ref[...], other_ref[...], dims, preferred_element_type=jnp.float32
    )
    top = jnp.max(logits, axis=0, keepdims=True)
    shifted = logits - top
    weights = jnp.exp(shifted)
    vocab_ids = lax.broadcasted_iota(jnp.int32, logits.shape, 0)
    target = jnp.sum(jnp.where(vocab_ids == ids_ref[...], logits, 0.0), axis=0, keepdims=True)
    out_ref[0:1, :] = top
    out_ref[1:2, :] = jnp.sum(weights, axis=0, keepdims=True)
    out_ref[2:3, :] = jnp.sum(weights * shifted, axis=0, keepdims=True)
    out_ref[3:4, :] = target
    out_ref[4:8, :] = jnp.zeros((4, top.shape[1]), jnp.float32)


def row_stats(ids, rows_mine, rows_other, emb_mine, emb_other, tile=512):
    n_rows, feat = rows_mine.shape
    vocab = emb_mine.shape[0]
    return pl.pallas_call(
        stats_kernel,
        grid=(n_rows // tile,),
        in_specs=[
            pl.BlockSpec((1, tile), lambda i: (0, i)),
            pl.BlockSpec((tile, feat), lambda i: (i, 0)),
            pl.BlockSpec((tile, feat), lambda i: (i, 0)),
            pl.BlockSpec((vocab, feat), lambda i: (0, 0)),
            pl.BlockSpec((vocab, feat), lambda i: (0, 0)),
        ],
        out_specs=pl.BlockSpec((8, tile), lambda i: (0, i)),
        out_shape=jax.ShapeDtypeStruct((8, n_rows), jnp.float32),
    )(ids, rows_mine, rows_other, emb_mine, emb_other)


def shards(n_voc, hidden, gain, embedding, targets, span_start, span_len, deal_order):
    per_dev = hidden.shape[0]
    slot_len = hidden.shape[1]
    width = hidden.shape[2]
    total = deal_order.shape[0]
    n_req = total // per_dev
    voc_local = embedding.shape[0]
    piece = voc_local // n_req
    half = width // 2
    here = lax.axis_index("req")
    vhere = lax.axis_index("vocab")
    core = vhere % 2
    positions = jnp.arange(total, dtype=jnp.int32)
    source_of = jnp.sum(
        jnp.where(deal_order[None, :] == positions[:, None], positions[None, :], 0), axis=1
    )

    emb_piece = lax.all_to_all(embedding, "req", split_axis=0, concat_axis=1, tiled=True)

    wide = hidden.astype(jnp.float32)
    scale = lax.rsqrt(jnp.mean(wide * wide, axis=-1, keepdims=True) + eps)
    half_rows = lax.dynamic_slice_in_dim(hidden, core * half, half, axis=2).astype(jnp.float32)
    half_gain = lax.dynamic_slice_in_dim(gain, core * half, half)
    my_half = (half_rows * scale * half_gain).astype(jnp.bfloat16)
    block = slot_len // n_req
    digits = jnp.stack([targets // 16384, (targets // 128) % 128, targets % 128], axis=1)
    bounds = jnp.zeros((per_dev, 1, slot_len), jnp.int32)
    bounds = bounds.at[:, 0, 0].set(span_start).at[:, 0, 1].set(span_len)
    meta = jnp.concatenate([digits, bounds], axis=1).astype(jnp.bfloat16).reshape(per_dev, 1, 1, -1)
    meta = jnp.pad(meta, ((0, 0), (0, 0), (0, 0), (0, half - meta.shape[3])))
    blocks = jnp.concatenate(
        [my_half.reshape(per_dev, n_req, block, half), jnp.broadcast_to(meta, (per_dev, n_req, 1, half))],
        axis=2,
    ).transpose(1, 0, 2, 3)
    received = lax.all_to_all(blocks, "req", split_axis=0, concat_axis=0, tiled=True)
    spread_rows = received[:, :, :block].reshape(total, block, half)
    meta_all = received[:, :, block, : 4 * slot_len].astype(jnp.int32).reshape(total, 4, slot_len)
    all_targets = meta_all[:, 0] * 16384 + meta_all[:, 1] * 128 + meta_all[:, 2]
    all_starts = meta_all[:, 3, 0]
    all_lengths = meta_all[:, 3, 1]
    dealt_rows = jnp.take(spread_rows, source_of, axis=0)
    home_rows = lax.all_to_all(dealt_rows, "req", split_axis=0, concat_axis=1, tiled=True)

    my_slots = here * per_dev + jnp.arange(per_dev, dtype=jnp.int32)
    members = jnp.take(source_of, my_slots)
    lengths = jnp.take(all_lengths, members)
    starts = jnp.take(all_starts, members)
    row_base = jnp.arange(per_dev, dtype=jnp.int32) * slot_len + starts
    row_index, in_span = compact_plan(row_base, lengths, CAP)
    safe_index = jnp.where(in_span, row_index, 0)
    compact_half = jnp.take(home_rows.reshape(per_dev * slot_len, half), safe_index, axis=0)

    rows_mine = lax.all_gather(compact_half, "req", axis=0, tiled=True)
    pairs = [(2 * k + j, 2 * k + 1 - j) for k in range(n_voc // 2) for j in range(2)]
    rows_other = lax.ppermute(rows_mine, "vocab", pairs)

    emb_mine = lax.dynamic_slice_in_dim(emb_piece, core * half, half, axis=1)
    emb_other = lax.dynamic_slice_in_dim(emb_piece, (1 - core) * half, half, axis=1)
    dealt_members = source_of.reshape(n_req, per_dev)
    dealt_lengths = jnp.take(all_lengths, dealt_members)
    dealt_offsets = jnp.cumsum(dealt_lengths, axis=1) - dealt_lengths
    dealt_starts = jnp.take(all_starts, dealt_members)
    member_targets = jnp.take(all_targets, source_of, axis=0).reshape(n_req, per_dev, slot_len)
    counter = jnp.arange(CAP, dtype=jnp.int32)
    source_pos = counter[None, None, :] - dealt_offsets[:, :, None] + dealt_starts[:, :, None]
    in_member = (counter[None, None, :] >= dealt_offsets[:, :, None]) & (
        counter[None, None, :] < (dealt_offsets + dealt_lengths)[:, :, None]
    )
    slot_ids = jnp.arange(slot_len, dtype=jnp.int32)
    hit = (source_pos[..., None] == slot_ids) & in_member[..., None]
    target_ids = jnp.sum(jnp.where(hit, member_targets[:, :, None, :], 0), axis=(1, 3)).reshape(-1)

    local_ids = (target_ids - (vhere * voc_local + here * piece)).reshape(1, -1)
    local_stats = row_stats(local_ids, rows_mine, rows_other, emb_mine, emb_other)[:4]

    def merge(stats):
        top_each, mass_each, spread_each, target_each = stats[:, 0], stats[:, 1], stats[:, 2], stats[:, 3]
        top = jnp.max(top_each, axis=0)
        gap = top_each - top[None]
        factor = jnp.exp(gap)
        mass = jnp.sum(factor * mass_each, axis=0)
        spread = jnp.sum(factor * (spread_each + gap * mass_each), axis=0)
        return jnp.stack([top, mass, spread, jnp.sum(target_each, axis=0)])

    offsets = dealt_offsets.reshape(-1)
    pos = jnp.arange(slot_len, dtype=jnp.int32)[None, :]
    local_stats = local_stats.reshape(4, n_req, CAP)
    request_rows = jnp.take(local_stats, deal_order // per_dev, axis=1)
    at = (jnp.take(offsets, deal_order) - all_starts)[:, None] + pos
    pick = (jnp.arange(CAP, dtype=jnp.int32)[None, :, None] == at[:, None, :]).astype(jnp.float32)
    picked = lax.dot_general(
        request_rows.transpose(1, 0, 2),
        pick,
        (((2,), (1,)), ((0,), (0,))),
        precision=lax.Precision.HIGHEST,
        preferred_element_type=jnp.float32,
    )
    to_home = picked.reshape(n_req, per_dev, 4, slot_len).transpose(0, 2, 1, 3)
    to_all = jnp.broadcast_to(to_home[:, None], (n_req, n_voc) + to_home.shape[1:])
    to_all = to_all.reshape((n_req * n_voc,) + to_home.shape[1:])
    from_all = lax.all_to_all(to_all, ("req", "vocab"), split_axis=0, concat_axis=0, tiled=True)
    row_top, row_mass, row_spread, row_target = merge(from_all)
    log_mass = jnp.log(row_mass)

    my_reqs = here * per_dev + jnp.arange(per_dev, dtype=jnp.int32)
    my_start = jnp.take(all_starts, my_reqs)
    my_len = jnp.take(all_lengths, my_reqs)
    inside = (pos >= my_start[:, None]) & (pos < (my_start + my_len)[:, None])
    out_logprob = jnp.where(inside, row_target - row_top - log_mass, 0.0)
    out_entropy = jnp.where(inside, log_mass - row_spread / row_mass, 0.0)
    return (out_logprob, out_entropy)


def solution(mesh):
    in_specs = (
        P("req", None, None),
        P(),
        P("vocab", "req"),
        P("req", None),
        P("req"),
        P("req"),
        P(),
    )
    out_specs = (P("req", None), P("req", None))
    body = functools.partial(shards, mesh.shape["vocab"])
    return jax.shard_map(body, mesh=mesh, in_specs=in_specs, out_specs=out_specs, check_vma=False)
```

```python
import functools

import jax
import jax.numpy as jnp
from jax import lax
from jax.sharding import PartitionSpec as P
from jax.experimental import pallas as pl

CAP = 224


eps = 1e-06


def compact_plan(row_base, lengths, capacity):
    offsets = jnp.cumsum(lengths) - lengths
    counter = jnp.arange(capacity, dtype=jnp.int32)
    member = jnp.sum((counter[:, None] >= offsets[None, :]).astype(jnp.int32), axis=1) - 1
    member_hot = (member[:, None] == jnp.arange(lengths.shape[0], dtype=jnp.int32)[None, :]).astype(
        jnp.int32
    )
    row_index = jnp.sum(member_hot * (row_base - offsets)[None, :], axis=1) + counter
    in_span = counter < jnp.sum(lengths)
    return (row_index, in_span)


def normalize(rows, gain):
    wide_rows = rows.astype(jnp.float32)
    scale = lax.rsqrt(jnp.mean(wide_rows * wide_rows, axis=-1, keepdims=True) + eps)
    return (wide_rows * scale * gain).astype(jnp.bfloat16)


def gather_by_all_to_all(x, axis, n):
    tiles = jnp.broadcast_to(x[None], (n,) + x.shape)
    return lax.all_to_all(tiles, axis, split_axis=0, concat_axis=0, tiled=True)


def stats_kernel(ids_ref, mine_ref, other_ref, emb_mine_ref, emb_other_ref, out_ref):
    dims = (((1,), (1,)), ((), ()))
    logits = lax.dot_general(emb_mine_ref[...], mine_ref[...], dims, preferred_element_type=jnp.float32)
    logits = logits + lax.dot_general(
        emb_other_ref[...], other_ref[...], dims, preferred_element_type=jnp.float32
    )
    top = jnp.max(logits, axis=0, keepdims=True)
    shifted = logits - top
    weights = jnp.exp(shifted)
    vocab_ids = lax.broadcasted_iota(jnp.int32, logits.shape, 0)
    target = jnp.sum(jnp.where(vocab_ids == ids_ref[...], logits, 0.0), axis=0, keepdims=True)
    out_ref[0:1, :] = top
    out_ref[1:2, :] = jnp.sum(weights, axis=0, keepdims=True)
    out_ref[2:3, :] = jnp.sum(weights * shifted, axis=0, keepdims=True)
    out_ref[3:4, :] = target
    out_ref[4:8, :] = jnp.zeros((4, top.shape[1]), jnp.float32)


def row_stats(ids, rows_mine, rows_other, emb_mine, emb_other, tile=512):
    n_rows, feat = rows_mine.shape
    vocab = emb_mine.shape[0]
    return pl.pallas_call(
        stats_kernel,
        grid=(n_rows // tile,),
        in_specs=[
            pl.BlockSpec((1, tile), lambda i: (0, i)),
            pl.BlockSpec((tile, feat), lambda i: (i, 0)),
            pl.BlockSpec((tile, feat), lambda i: (i, 0)),
            pl.BlockSpec((vocab, feat), lambda i: (0, 0)),
            pl.BlockSpec((vocab, feat), lambda i: (0, 0)),
        ],
        out_specs=pl.BlockSpec((8, tile), lambda i: (0, i)),
        out_shape=jax.ShapeDtypeStruct((8, n_rows), jnp.float32),
    )(ids, rows_mine, rows_other, emb_mine, emb_other)


def shards(n_voc, hidden, gain, embedding, targets, span_start, span_len, deal_order):
    per_dev = hidden.shape[0]
    slot_len = hidden.shape[1]
    width = hidden.shape[2]
    total = deal_order.shape[0]
    n_req = total // per_dev
    voc_local = embedding.shape[0]
    piece = voc_local // n_req
    half = width // 2
    here = lax.axis_index("req")
    vhere = lax.axis_index("vocab")
    core = vhere % 2
    positions = jnp.arange(total, dtype=jnp.int32)
    source_of = jnp.sum(
        jnp.where(deal_order[None, :] == positions[:, None], positions[None, :], 0), axis=1
    )

    emb_piece = lax.all_to_all(embedding, "req", split_axis=0, concat_axis=1, tiled=True)

    wide = hidden.astype(jnp.float32)
    scale = lax.rsqrt(jnp.mean(wide * wide, axis=-1, keepdims=True) + eps)
    half_rows = lax.dynamic_slice_in_dim(hidden, core * half, half, axis=2).astype(jnp.float32)
    half_gain = lax.dynamic_slice_in_dim(gain, core * half, half)
    my_half = (half_rows * scale * half_gain).astype(jnp.bfloat16)
    block = slot_len // n_req
    digits = jnp.stack([targets // 16384, (targets // 128) % 128, targets % 128], axis=1)
    bounds = jnp.concatenate(
        [span_start[:, None], span_len[:, None], jnp.zeros((per_dev, slot_len - 2), jnp.int32)], axis=1
    )[:, None, :]
    meta = jnp.concatenate([digits, bounds], axis=1).astype(jnp.bfloat16).reshape(per_dev, 1, 1, -1)
    meta = jnp.pad(meta, ((0, 0), (0, 0), (0, 0), (0, half - meta.shape[3])))
    blocks = jnp.concatenate(
        [my_half.reshape(per_dev, n_req, block, half), jnp.broadcast_to(meta, (per_dev, n_req, 1, half))],
        axis=2,
    ).transpose(1, 0, 2, 3)
    received = lax.all_to_all(blocks, "req", split_axis=0, concat_axis=0, tiled=True)
    spread_rows = received[:, :, :block].reshape(total, block, half)
    meta_all = received[:, :, block, : 4 * slot_len].astype(jnp.int32).reshape(total, 4, slot_len)
    all_targets = meta_all[:, 0] * 16384 + meta_all[:, 1] * 128 + meta_all[:, 2]
    all_starts = meta_all[:, 3, 0]
    all_lengths = meta_all[:, 3, 1]
    dealt_rows = jnp.take(spread_rows, source_of, axis=0)
    home_rows = lax.all_to_all(dealt_rows, "req", split_axis=0, concat_axis=1, tiled=True)

    my_slots = here * per_dev + jnp.arange(per_dev, dtype=jnp.int32)
    members = jnp.take(source_of, my_slots)
    lengths = jnp.take(all_lengths, members)
    starts = jnp.take(all_starts, members)
    row_base = jnp.arange(per_dev, dtype=jnp.int32) * slot_len + starts
    row_index, in_span = compact_plan(row_base, lengths, CAP)
    safe_index = jnp.where(in_span, row_index, 0)
    compact_half = jnp.take(home_rows.reshape(per_dev * slot_len, half), safe_index, axis=0)

    rows_mine = lax.all_gather(compact_half, "req", axis=0, tiled=True)
    pairs = [(2 * k + j, 2 * k + 1 - j) for k in range(n_voc // 2) for j in range(2)]
    rows_other = lax.ppermute(rows_mine, "vocab", pairs)

    emb_mine = lax.dynamic_slice_in_dim(emb_piece, core * half, half, axis=1)
    emb_other = lax.dynamic_slice_in_dim(emb_piece, (1 - core) * half, half, axis=1)
    dealt_members = source_of.reshape(n_req, per_dev)
    dealt_lengths = jnp.take(all_lengths, dealt_members)
    dealt_offsets = jnp.cumsum(dealt_lengths, axis=1) - dealt_lengths
    dealt_starts = jnp.take(all_starts, dealt_members)
    member_targets = jnp.take(all_targets, source_of, axis=0).reshape(n_req, per_dev, slot_len)
    counter = jnp.arange(CAP, dtype=jnp.int32)
    source_pos = counter[None, None, :] - dealt_offsets[:, :, None] + dealt_starts[:, :, None]
    in_member = (counter[None, None, :] >= dealt_offsets[:, :, None]) & (
        counter[None, None, :] < (dealt_offsets + dealt_lengths)[:, :, None]
    )
    slot_ids = jnp.arange(slot_len, dtype=jnp.int32)
    hit = (source_pos[..., None] == slot_ids) & in_member[..., None]
    target_ids = jnp.sum(jnp.where(hit, member_targets[:, :, None, :], 0), axis=(1, 3)).reshape(-1)

    local_ids = (target_ids - (vhere * voc_local + here * piece)).reshape(1, -1)
    local_stats = row_stats(local_ids, rows_mine, rows_other, emb_mine, emb_other)[:4]

    def merge(stats):
        top_each, mass_each, spread_each, target_each = stats[:, 0], stats[:, 1], stats[:, 2], stats[:, 3]
        top = jnp.max(top_each, axis=0)
        gap = top_each - top[None]
        factor = jnp.exp(gap)
        mass = jnp.sum(factor * mass_each, axis=0)
        spread = jnp.sum(factor * (spread_each + gap * mass_each), axis=0)
        return jnp.stack([top, mass, spread, jnp.sum(target_each, axis=0)])

    offsets = dealt_offsets.reshape(-1)
    pos = jnp.arange(slot_len, dtype=jnp.int32)[None, :]
    local_stats = local_stats.reshape(4, n_req, CAP)
    request_rows = jnp.take(local_stats, deal_order // per_dev, axis=1)
    at = (jnp.take(offsets, deal_order) - all_starts)[:, None] + pos
    pick = (jnp.arange(CAP, dtype=jnp.int32)[None, :, None] == at[:, None, :]).astype(jnp.float32)
    picked = lax.dot_general(
        request_rows.transpose(1, 0, 2),
        pick,
        (((2,), (1,)), ((0,), (0,))),
        precision=lax.Precision.HIGHEST,
        preferred_element_type=jnp.float32,
    )
    to_home = picked.reshape(n_req, per_dev, 4, slot_len).transpose(0, 2, 1, 3)
    by_req = merge(lax.all_to_all(to_home, "req", split_axis=0, concat_axis=0, tiled=True))
    row_top, row_mass, row_spread, row_target = merge(gather_by_all_to_all(by_req, "vocab", n_voc))
    log_mass = jnp.log(row_mass)

    my_reqs = here * per_dev + jnp.arange(per_dev, dtype=jnp.int32)
    my_start = jnp.take(all_starts, my_reqs)
    my_len = jnp.take(all_lengths, my_reqs)
    inside = (pos >= my_start[:, None]) & (pos < (my_start + my_len)[:, None])
    out_logprob = jnp.where(inside, row_target - row_top - log_mass, 0.0)
    out_entropy = jnp.where(inside, log_mass - row_spread / row_mass, 0.0)
    return (out_logprob, out_entropy)


def solution(mesh):
    in_specs = (
        P("req", None, None),
        P(),
        P("vocab", "req"),
        P("req", None),
        P("req"),
        P("req"),
        P(),
    )
    out_specs = (P("req", None), P("req", None))
    body = functools.partial(shards, mesh.shape["vocab"])
    return jax.shard_map(body, mesh=mesh, in_specs=in_specs, out_specs=out_specs, check_vma=False)
```

```python
import functools

import jax
import jax.numpy as jnp
from jax import lax
from jax.sharding import PartitionSpec as P
from jax.experimental import pallas as pl

CAP = 224


eps = 1e-06


def compact_plan(row_base, lengths, capacity):
    offsets = jnp.cumsum(lengths) - lengths
    counter = jnp.arange(capacity, dtype=jnp.int32)
    member = jnp.sum((counter[:, None] >= offsets[None, :]).astype(jnp.int32), axis=1) - 1
    member_hot = (member[:, None] == jnp.arange(lengths.shape[0], dtype=jnp.int32)[None, :]).astype(
        jnp.int32
    )
    row_index = jnp.sum(member_hot * (row_base - offsets)[None, :], axis=1) + counter
    in_span = counter < jnp.sum(lengths)
    return (row_index, in_span)


def normalize(rows, gain):
    wide_rows = rows.astype(jnp.float32)
    scale = lax.rsqrt(jnp.mean(wide_rows * wide_rows, axis=-1, keepdims=True) + eps)
    return (wide_rows * scale * gain).astype(jnp.bfloat16)


def gather_by_all_to_all(x, axis, n):
    tiles = jnp.broadcast_to(x[None], (n,) + x.shape)
    return lax.all_to_all(tiles, axis, split_axis=0, concat_axis=0, tiled=True)


def stats_kernel(ids_ref, mine_ref, other_ref, emb_mine_ref, emb_other_ref, out_ref):
    dims = (((1,), (1,)), ((), ()))
    logits = lax.dot_general(emb_mine_ref[...], mine_ref[...], dims, preferred_element_type=jnp.float32)
    logits = logits + lax.dot_general(
        emb_other_ref[...], other_ref[...], dims, preferred_element_type=jnp.float32
    )
    top = jnp.max(logits, axis=0, keepdims=True)
    shifted = logits - top
    weights = jnp.exp(shifted)
    vocab_ids = lax.broadcasted_iota(jnp.int32, logits.shape, 0)
    target = jnp.sum(jnp.where(vocab_ids == ids_ref[...], logits, 0.0), axis=0, keepdims=True)
    out_ref[0:1, :] = top
    out_ref[1:2, :] = jnp.sum(weights, axis=0, keepdims=True)
    out_ref[2:3, :] = jnp.sum(weights * shifted, axis=0, keepdims=True)
    out_ref[3:4, :] = target


def row_stats(ids, rows_mine, rows_other, emb_mine, emb_other, tile=512):
    n_rows, feat = rows_mine.shape
    vocab = emb_mine.shape[0]
    return pl.pallas_call(
        stats_kernel,
        grid=(n_rows // tile,),
        in_specs=[
            pl.BlockSpec((1, tile), lambda i: (0, i)),
            pl.BlockSpec((tile, feat), lambda i: (i, 0)),
            pl.BlockSpec((tile, feat), lambda i: (i, 0)),
            pl.BlockSpec((vocab, feat), lambda i: (0, 0)),
            pl.BlockSpec((vocab, feat), lambda i: (0, 0)),
        ],
        out_specs=pl.BlockSpec((4, tile), lambda i: (0, i)),
        out_shape=jax.ShapeDtypeStruct((4, n_rows), jnp.float32),
    )(ids, rows_mine, rows_other, emb_mine, emb_other)


def shards(n_voc, hidden, gain, embedding, targets, span_start, span_len, deal_order):
    per_dev = hidden.shape[0]
    slot_len = hidden.shape[1]
    width = hidden.shape[2]
    total = deal_order.shape[0]
    n_req = total // per_dev
    voc_local = embedding.shape[0]
    piece = voc_local // n_req
    half = width // 2
    here = lax.axis_index("req")
    vhere = lax.axis_index("vocab")
    core = vhere % 2
    positions = jnp.arange(total, dtype=jnp.int32)
    source_of = jnp.sum(
        jnp.where(deal_order[None, :] == positions[:, None], positions[None, :], 0), axis=1
    )

    emb_piece = lax.all_to_all(embedding, "req", split_axis=0, concat_axis=1, tiled=True)

    wide = hidden.astype(jnp.float32)
    scale = lax.rsqrt(jnp.mean(wide * wide, axis=-1, keepdims=True) + eps)
    half_rows = lax.dynamic_slice_in_dim(hidden, core * half, half, axis=2).astype(jnp.float32)
    half_gain = lax.dynamic_slice_in_dim(gain, core * half, half)
    my_half = (half_rows * scale * half_gain).astype(jnp.bfloat16)
    block = slot_len // n_req
    digits = jnp.stack([targets // 16384, (targets // 128) % 128, targets % 128], axis=1)
    bounds = jnp.zeros((per_dev, 1, slot_len), jnp.int32)
    bounds = bounds.at[:, 0, 0].set(span_start).at[:, 0, 1].set(span_len)
    meta = jnp.concatenate([digits, bounds], axis=1).astype(jnp.bfloat16).reshape(per_dev, 1, 1, -1)
    meta = jnp.pad(meta, ((0, 0), (0, 0), (0, 0), (0, half - meta.shape[3])))
    blocks = jnp.concatenate(
        [my_half.reshape(per_dev, n_req, block, half), jnp.broadcast_to(meta, (per_dev, n_req, 1, half))],
        axis=2,
    ).transpose(1, 0, 2, 3)
    received = lax.all_to_all(blocks, "req", split_axis=0, concat_axis=0, tiled=True)
    spread_rows = received[:, :, :block].reshape(total, block, half)
    meta_all = received[:, :, block, : 4 * slot_len].astype(jnp.int32).reshape(total, 4, slot_len)
    all_targets = meta_all[:, 0] * 16384 + meta_all[:, 1] * 128 + meta_all[:, 2]
    all_starts = meta_all[:, 3, 0]
    all_lengths = meta_all[:, 3, 1]
    dealt_rows = jnp.take(spread_rows, source_of, axis=0)
    home_rows = lax.all_to_all(dealt_rows, "req", split_axis=0, concat_axis=1, tiled=True)

    my_slots = here * per_dev + jnp.arange(per_dev, dtype=jnp.int32)
    members = jnp.take(source_of, my_slots)
    lengths = jnp.take(all_lengths, members)
    starts = jnp.take(all_starts, members)
    row_base = jnp.arange(per_dev, dtype=jnp.int32) * slot_len + starts
    row_index, in_span = compact_plan(row_base, lengths, CAP)
    safe_index = jnp.where(in_span, row_index, 0)
    compact_half = jnp.take(home_rows.reshape(per_dev * slot_len, half), safe_index, axis=0)

    rows_mine = lax.all_gather(compact_half, "req", axis=0, tiled=True)
    pairs = [(2 * k + j, 2 * k + 1 - j) for k in range(n_voc // 2) for j in range(2)]
    rows_other = lax.ppermute(rows_mine, "vocab", pairs)

    emb_mine = lax.dynamic_slice_in_dim(emb_piece, core * half, half, axis=1)
    emb_other = lax.dynamic_slice_in_dim(emb_piece, (1 - core) * half, half, axis=1)
    dealt_members = source_of.reshape(n_req, per_dev)
    dealt_lengths = jnp.take(all_lengths, dealt_members)
    dealt_offsets = jnp.cumsum(dealt_lengths, axis=1) - dealt_lengths
    dealt_starts = jnp.take(all_starts, dealt_members)
    member_targets = jnp.take(all_targets, source_of, axis=0).reshape(n_req, per_dev, slot_len)
    counter = jnp.arange(CAP, dtype=jnp.int32)
    source_pos = counter[None, None, :] - dealt_offsets[:, :, None] + dealt_starts[:, :, None]
    in_member = (counter[None, None, :] >= dealt_offsets[:, :, None]) & (
        counter[None, None, :] < (dealt_offsets + dealt_lengths)[:, :, None]
    )
    slot_ids = jnp.arange(slot_len, dtype=jnp.int32)
    hit = (source_pos[..., None] == slot_ids) & in_member[..., None]
    target_ids = jnp.sum(jnp.where(hit, member_targets[:, :, None, :], 0), axis=(1, 3)).reshape(-1)

    local_ids = (target_ids - (vhere * voc_local + here * piece)).reshape(1, -1)
    local_stats = row_stats(local_ids, rows_mine, rows_other, emb_mine, emb_other)

    def merge(stats):
        top_each, mass_each, spread_each, target_each = stats[:, 0], stats[:, 1], stats[:, 2], stats[:, 3]
        top = jnp.max(top_each, axis=0)
        gap = top_each - top[None]
        factor = jnp.exp(gap)
        mass = jnp.sum(factor * mass_each, axis=0)
        spread = jnp.sum(factor * (spread_each + gap * mass_each), axis=0)
        return jnp.stack([top, mass, spread, jnp.sum(target_each, axis=0)])

    offsets = dealt_offsets.reshape(-1)
    pos = jnp.arange(slot_len, dtype=jnp.int32)[None, :]
    local_stats = local_stats.reshape(4, n_req, CAP)
    request_rows = jnp.take(local_stats, deal_order // per_dev, axis=1)
    at = (jnp.take(offsets, deal_order) - all_starts)[:, None] + pos
    pick = (jnp.arange(CAP, dtype=jnp.int32)[None, :, None] == at[:, None, :]).astype(jnp.float32)
    picked = lax.dot_general(
        request_rows.transpose(1, 0, 2),
        pick,
        (((2,), (1,)), ((0,), (0,))),
        precision=lax.Precision.HIGHEST,
        preferred_element_type=jnp.float32,
    )
    to_home = picked.reshape(n_req, per_dev, 4, slot_len).transpose(0, 2, 1, 3)
    by_req = merge(lax.all_to_all(to_home, "req", split_axis=0, concat_axis=0, tiled=True))
    row_top, row_mass, row_spread, row_target = merge(gather_by_all_to_all(by_req, "vocab", n_voc))
    log_mass = jnp.log(row_mass)

    my_reqs = here * per_dev + jnp.arange(per_dev, dtype=jnp.int32)
    my_start = jnp.take(all_starts, my_reqs)
    my_len = jnp.take(all_lengths, my_reqs)
    inside = (pos >= my_start[:, None]) & (pos < (my_start + my_len)[:, None])
    out_logprob = jnp.where(inside, row_target - row_top - log_mass, 0.0)
    out_entropy = jnp.where(inside, log_mass - row_spread / row_mass, 0.0)
    return (out_logprob, out_entropy)


def solution(mesh):
    in_specs = (
        P("req", None, None),
        P(),
        P("vocab", "req"),
        P("req", None),
        P("req"),
        P("req"),
        P(),
    )
    out_specs = (P("req", None), P("req", None))
    body = functools.partial(shards, mesh.shape["vocab"])
    return jax.shard_map(body, mesh=mesh, in_specs=in_specs, out_specs=out_specs, check_vma=False)
```
